32 devices in a mesh: prow: 8 (over z, x), pcol: 4 (over y, core).
Axes of the slice: x: 2, y: 2, z: 4, core: 2. Of those that a mesh axis runs over, the one named last changes fastest.
Arguments:
- dof_values: float32 [9, 56, 4096], P(None, None, ('prow', 'pcol')), may hold values from -6 to 6
- grad_matrix: float32 [3, 56, 56], replicated, may hold values from -0.75 to 0.75
- stiff_matrix: float32 [3, 56, 56], replicated, may hold values from -0.1875 to 0.1875
- face_proj: float32 [4, 21, 56], replicated, may hold values from -0.75 to 0.75
- face_lift: float32 [4, 56, 21], replicated, may hold values from -0.3125 to 0.3125
- rotate: float32 [3, 21, 21], replicated, may hold values from -1.25 to 1.25
- material: float32 [16, 3], replicated, may hold values from 0.5 to 2
- material_id: int32 [4096], P(('prow', 'pcol')), may hold values from 0 to 15
- inv_jacobian: float32 [3, 3, 4096], P(None, None, ('prow', 'pcol')), may hold values from -3 to 3
- normals: float32 [4, 3, 4096], P(None, None, ('prow', 'pcol')), may hold values from -2 to 2
- orientation: int32 [4, 4096], P(None, ('prow', 'pcol')), may hold values from 0 to 2
- neighbour: int32 [4, 4096], P(None, ('prow', 'pcol')), may hold values from -1 to 127, as said below
- neighbour_face: int32 [4, 4096], P(None, ('prow', 'pcol')), may hold values from 0 to 3, as said below
- send_list: int32 [8, 4, 8, 24], P('prow', 'pcol'), may hold values from -1 to 511, as said below
- recv_list: int32 [8, 4, 8, 24], P('prow', 'pcol'), may hold values from -1 to 511, as said below
Outputs:
- new_dofs: float32 [9, 56, 4096], P(None, None, ('prow', 'pcol'))
The draws below stay inside these ranges and needn't reach their ends.
Inputs may be any that keep to these rules, and one draw needn't show every extreme that they name: `neighbour`: -1 where the face has no neighbour in the same partition; otherwise faces are matched in pairs: the element neighbour[f, e] lists e back across its face neighbour_face[f, e]. `neighbour_face`: 0 where neighbour is -1. `send_list`: entry (r, c, d, m) is a local face id of partition (r, c) whose neighbour lies in the partition at offset d, or -1; live slots of a direction come first, each such face appears once, and the live count of (r, c, d) equals that of the partner's direction 7 - d; directions leaving the grid have none. Some partition has 24 live slots in all eight directions, and every live count is at most 24. `recv_list`: entry (r, c, d, m) is the local face id of partition (r, c) that meets the face in slot m of the send_list of the partner at offset d for direction 7 - d, or -1 where that slot is empty; its live slots hold the same faces as send_list of (r, c, d) in another order.
All inputs are finite; a program needn't handle non-finite values.
Results may differ from the reference program's by a relative error of at most 0.0003.
Values sent between devices are 32-bit elements; how exact they have to be, the bound alone decides.
No kernel may reach another device: no remote copies, remote signals or barrier semaphores. Data moves between devices by JAX's collectives and lax.ppermute only.
A program may use at most 64 MiB of HBM per device.

```python
import math
import jax
import jax.numpy as jnp
from jax import lax

BASIS = 56
FACE_BASIS = 21
QUANT = 9
ORDER = 6
STEPS = 2
MATERIALS = 16
E_DEV = 128
PEER_CAP = 24
E = 4096
N_PROW = 8
N_PCOL = 4


OFFSETS = ((-1, -1), (-1, 0), (-1, 1), (0, -1), (0, 1), (1, -1), (1, 0), (1, 1))


def link_tables(key):
    row_count = N_PROW
    col_count = N_PCOL
    face_count = 4 * E_DEV
    devices = row_count * col_count
    key = jax.random.fold_in(key, 9173)
    key_count, key_turn, key_hub_row, key_hub_col, key_perm = jax.random.split(key, 5)
    link_raw = jax.random.randint(key_count, (row_count, col_count, 8), (PEER_CAP + 3) // 4, PEER_CAP + 1)
    turn_raw = jax.random.randint(key_turn, (row_count, col_count, 8), 0, PEER_CAP)
    hub_row = jax.random.randint(key_hub_row, (), 1, row_count - 1)
    hub_col = jax.random.randint(key_hub_col, (), 1, col_count - 1)
    row_ids = jnp.arange(row_count, dtype=jnp.int32)[:, None]
    col_ids = jnp.arange(col_count, dtype=jnp.int32)[None, :]
    link_planes = []
    for direction in range(8):
        link_plane = link_raw[:, :, direction]
        if direction >= 4:
            row_step, col_step = OFFSETS[direction]
            at_hub = (row_ids == hub_row) & (col_ids == hub_col)
            before_hub = (row_ids == hub_row - row_step) & (col_ids == hub_col - col_step)
            link_plane = jnp.where(at_hub | before_hub, PEER_CAP, link_plane)
        link_planes.append(link_plane)
    counts = []
    turns = []
    for direction in range(8):
        row_step, col_step = OFFSETS[direction]
        inside = (row_ids + row_step >= 0) & (row_ids + row_step < row_count) & (col_ids + col_step >= 0) & (col_ids + col_step < col_count)
        if direction >= 4:
            link_count = link_planes[direction]
            link_turn = -turn_raw[:, :, direction]
        else:
            link_count = jnp.roll(link_planes[7 - direction], (-row_step, -col_step), (0, 1))
            link_turn = jnp.roll(turn_raw[:, :, 7 - direction], (-row_step, -col_step), (0, 1))
        counts.append(jnp.where(inside, link_count, 0))
        turns.append(link_turn)
    counts = jnp.stack(counts, axis=2).reshape(devices, 8)
    turns = jnp.stack(turns, axis=2).reshape(devices, 8)
    device_keys = jax.random.split(key_perm, devices)
    face_order = jax.vmap(lambda dev_key: jax.random.permutation(dev_key, face_count))(device_keys).astype(jnp.int32)
    starts = jnp.cumsum(counts, axis=1) - counts
    boundary = jnp.sum(counts, axis=1)
    slot_ids = jnp.arange(PEER_CAP, dtype=jnp.int32)
    live_slot = slot_ids[None, None, :] < counts[:, :, None]
    places = jnp.minimum(starts[:, :, None] + slot_ids[None, None, :], face_count - 1).reshape(devices, 8 * PEER_CAP)
    send_table = jnp.take_along_axis(face_order, places, axis=1).reshape(devices, 8, PEER_CAP)
    send_table = jnp.where(live_slot, send_table, -1)
    live_span = jnp.maximum(counts, 1)[:, :, None]
    source = (slot_ids[None, None, :] + turns[:, :, None]) % live_span
    recv_table = jnp.take_along_axis(send_table, source, axis=2)
    recv_table = jnp.where(live_slot, recv_table, -1)
    positions = jnp.arange(face_count, dtype=jnp.int32)[None, :]
    partner = boundary[:, None] + jnp.bitwise_xor(positions - boundary[:, None], 1)
    paired = (positions >= boundary[:, None]) & (partner < face_count)
    partner_face = jnp.take_along_axis(face_order, jnp.clip(partner, 0, face_count - 1), axis=1)
    near_elem = jnp.where(paired, partner_face % E_DEV, -1)
    near_face = jnp.where(paired, partner_face // E_DEV, 0)
    neighbour_table = jax.vmap(lambda where_ids, vals: jnp.zeros((face_count,), jnp.int32).at[where_ids].set(vals))(face_order, near_elem)
    near_face_table = jax.vmap(lambda where_ids, vals: jnp.zeros((face_count,), jnp.int32).at[where_ids].set(vals))(face_order, near_face)
    neighbour_table = jnp.transpose(neighbour_table.reshape(devices, 4, E_DEV), (1, 0, 2)).reshape(4, devices * E_DEV)
    near_face_table = jnp.transpose(near_face_table.reshape(devices, 4, E_DEV), (1, 0, 2)).reshape(4, devices * E_DEV)
    send_table = send_table.reshape(row_count, col_count, 8, PEER_CAP)
    recv_table = recv_table.reshape(row_count, col_count, 8, PEER_CAP)
    return (neighbour_table, near_face_table, send_table, recv_table)


def draw_neighbour(key, part):
    return link_tables(key)[0]


def draw_neighbour_face(key, part):
    return link_tables(key)[1]


def draw_send_list(key, part):
    return link_tables(key)[2]


def draw_recv_list(key, part):
    return link_tables(key)[3]


def plant(values, stream_key, low, largest):
    dims = values.shape
    place = [jax.random.randint(jax.random.fold_in(stream_key, axis), (), 0, dims[axis]) for axis in range(len(dims))]
    values = values.at[tuple(place)].set(low)
    longest = dims.index(max(dims))
    place[longest] = (place[longest] + 1) % dims[longest]
    return values.at[tuple(place)].set(largest)


def shard_levels(stream_key, shape, cuts, low, largest):
    gain = 1.0
    for axis_at, shards_of in cuts:
        heights = jax.random.uniform(jax.random.fold_in(jax.random.fold_in(stream_key, 6), axis_at), (shards_of,), jnp.float32, low / len(cuts), largest / len(cuts))
        gain = gain * jnp.repeat(jnp.exp(heights), shape[axis_at] // shards_of).reshape((-1,) + (1,) * (len(shape) - 1 - axis_at))
    return gain


def centred(stream_key, dims, width, limit, shards=(), kind=jnp.bfloat16):
    values = jax.random.normal(stream_key, dims, jnp.float32) * width
    if len(shards) > 0:
        values = shard_levels(stream_key, dims, shards, -0.22, 0.18) * values
    return jnp.clip(values, min=-limit, max=limit).astype(kind)


def setup_inputs(seed: int = 0) -> dict:
    key_list = jax.random.split(jax.random.key(seed), 16)
    return {
        "dof_values": centred(key_list[0], (QUANT, BASIS, E), 1.0, 6.0, ((2, 32),), jnp.float32),
        "grad_matrix": centred(key_list[1], (3, BASIS, BASIS), BASIS ** -0.5, 0.75, (), jnp.float32),
        "stiff_matrix": centred(key_list[2], (3, BASIS, BASIS), (16 * BASIS) ** -0.5, 0.1875, (), jnp.float32),
        "face_proj": centred(key_list[3], (4, FACE_BASIS, BASIS), BASIS ** -0.5, 0.75, (), jnp.float32),
        "face_lift": centred(key_list[4], (4, BASIS, FACE_BASIS), (16 * FACE_BASIS) ** -0.5, 0.3125, (), jnp.float32),
        "rotate": centred(key_list[5], (3, FACE_BASIS, FACE_BASIS), FACE_BASIS ** -0.5, 1.25, (), jnp.float32),
        "material": jnp.clip(jnp.exp(jax.random.uniform(key_list[6], (MATERIALS, 3), jnp.float32, math.log(0.5), math.log(2.0))), 0.5, 2.0),
        "material_id": plant(jax.random.randint(key_list[7], (E,), 0, MATERIALS), jax.random.fold_in(key_list[7], 1), 0, MATERIALS - 1).astype(jnp.int32),
        "inv_jacobian": centred(key_list[8], (3, 3, E), 0.5, 3.0, ((2, 32),), jnp.float32),
        "normals": centred(key_list[9], (4, 3, E), 0.3, 2.0, ((2, 32),), jnp.float32),
        "orientation": plant(jax.random.randint(key_list[10], (4, E), 0, 3), jax.random.fold_in(key_list[10], 1), 0, 2).astype(jnp.int32),
        "neighbour": draw_neighbour(jax.random.fold_in(key_list[15], 71), 0),
        "neighbour_face": draw_neighbour_face(jax.random.fold_in(key_list[15], 71), 0),
        "send_list": draw_send_list(jax.random.fold_in(key_list[15], 71), 0),
        "recv_list": draw_recv_list(jax.random.fold_in(key_list[15], 71), 0),
    }


exact_mode = lax.Precision.HIGHEST
time_step = 0.8
OFFSETS = ((-1, -1), (-1, 0), (-1, 1), (0, -1), (0, 1), (1, -1), (1, 0), (1, 1))
ENTRIES = ((0, 0, 6, 0), (0, 1, 6, 1), (0, 2, 6, 1), (0, 3, 7, 2), (0, 5, 8, 2), (0, 6, 0, 3), (0, 7, 3, 3), (0, 8, 5, 3), (1, 0, 7, 1), (1, 1, 7, 0), (1, 2, 7, 1), (1, 3, 6, 2), (1, 4, 8, 2), (1, 6, 3, 3), (1, 7, 1, 3), (1, 8, 4, 3), (2, 0, 8, 1), (2, 1, 8, 1), (2, 2, 8, 0), (2, 4, 7, 2), (2, 5, 6, 2), (2, 6, 5, 3), (2, 7, 4, 3), (2, 8, 2, 3))

def element_params(material, material_id, normals):
    id_range = jnp.arange(material.shape[0], dtype=jnp.int32)
    onehot = (material_id[None, :] == id_range[:, None]).astype(material.dtype)
    params = jnp.dot(material.T, onehot, precision=exact_mode)
    density, lame_first, shear_modulus = (params[0], params[1], params[2])
    values = (-(lame_first + 2.0 * shear_modulus), -lame_first, -shear_modulus, -1.0 / density)
    wave_speed = jnp.sqrt((lame_first + 2.0 * shear_modulus) / density) * lax.optimization_barrier(jnp.sum(jnp.abs(normals), axis=1))
    return (values, wave_speed)

def elastic_apply(parts, values):
    result = [None] * 9
    for comp_axis, row_index, col_index, kind_index in ENTRIES:
        term = values[kind_index] * parts[comp_axis][col_index]
        result[row_index] = term if result[row_index] is None else result[row_index] + term
    return jnp.stack(result, axis=0)

def star_apply(slopes, inv_jacobian, values):
    parts = [lax.optimization_barrier(jnp.sum(inv_jacobian[:, k][:, None, None, :] * slopes, axis=0)) for k in range(3)]
    return elastic_apply(parts, values)

def predict(current, inv_jacobian, values, grad_matrix):
    derivative = current
    integrated = time_step * current
    factor = time_step
    for power_level in range(1, ORDER):
        slopes = jnp.einsum('dab,qbe->dqae', grad_matrix, derivative, precision=exact_mode)
        derivative = -star_apply(slopes, inv_jacobian, values)
        factor = factor * time_step / (power_level + 1)
        integrated = integrated + factor * derivative
    return integrated

def local_part(current, inv_jacobian, values, grad_matrix, stiff_matrix, face_proj):
    integrated = predict(current, inv_jacobian, values, grad_matrix)
    slopes = jnp.einsum('dab,qbe->dqae', stiff_matrix, integrated, precision=exact_mode)
    volume = star_apply(slopes, inv_jacobian, values)
    face_data = jnp.einsum('fib,qbe->qife', face_proj, integrated, precision=exact_mode)
    return (volume, face_data)

def face_update(current, volume, face_data, neighbour_data, orientation, normals, values, wave_speed, rotate, face_lift):
    turned = jnp.einsum('hil,qlfe->hqife', rotate, neighbour_data, precision=exact_mode)
    chosen = (orientation[None] == jnp.arange(3, dtype=jnp.int32)[:, None, None]).astype(current.dtype)
    turned = lax.optimization_barrier(jnp.sum(turned * chosen[:, None, None, :, :], axis=0))
    both = face_data + turned
    apart = face_data - turned
    parts = [normals[:, k, :][None, None] * both for k in range(3)]
    flux_total = 0.5 * (elastic_apply(parts, values) + wave_speed[None, None] * apart)
    lifted = jnp.einsum('fai,pife->pae', face_lift, flux_total, precision=exact_mode)
    return current + volume - lifted

def reference(dof_values, grad_matrix, stiff_matrix, face_proj, face_lift, rotate, material, material_id, inv_jacobian, normals, orientation, neighbour, neighbour_face, send_list, recv_list):
    devices = N_PROW * N_PCOL

    def blocks(array):
        return jnp.moveaxis(array.reshape(array.shape[:-1] + (devices, E_DEV)), -2, 0)
    current = blocks(dof_values)
    mat_blocks = blocks(material_id)
    jac_blocks = blocks(inv_jacobian)
    normal_blocks = blocks(normals)
    orient_blocks = blocks(orientation)
    near_blocks = blocks(neighbour)
    near_face_blocks = blocks(neighbour_face)
    send_all = send_list.reshape(devices, 8, PEER_CAP)
    recv_all = recv_list.reshape(devices, 8, PEER_CAP)
    block_ids = jnp.arange(devices, dtype=jnp.int32)

    def block_local(inputs):
        block_state, block_material, block_jac, block_normals = inputs
        values, wave_speed = element_params(material, block_material, block_normals)
        return local_part(block_state, block_jac, values, grad_matrix, stiff_matrix, face_proj)
    for time_index in range(STEPS):
        volume, face_data = lax.map(block_local, (current, mat_blocks, jac_blocks, normal_blocks))
        flat_faces = face_data.reshape(devices, 9, FACE_BASIS, 4 * E_DEV)

        def block_update(inputs):
            block_id, block_state, block_volume, block_material, block_normals, block_orient, block_near, block_near_face, block_recv = inputs
            values, wave_speed = element_params(material, block_material, block_normals)
            own_faces = flat_faces[block_id]
            local_index = (block_near_face * E_DEV + jnp.maximum(block_near, 0)).reshape(-1)
            local_data = jnp.take(own_faces, local_index, axis=2)
            pieces = []
            for direction in range(8):
                row_step, col_step = OFFSETS[direction]
                partner = jnp.clip(block_id + row_step * N_PCOL + col_step, 0, devices - 1)
                source_ids = send_all[partner, 7 - direction]
                sent_data = jnp.take(flat_faces[partner], jnp.maximum(source_ids, 0), axis=2)
                pieces.append(sent_data * (source_ids >= 0).astype(own_faces.dtype))
            received = jnp.concatenate(pieces, axis=2)
            targets = jnp.where(block_recv >= 0, block_recv, 4 * E_DEV).reshape(-1)
            arrived = jnp.zeros_like(own_faces).at[:, :, targets].set(received, mode='drop')
            inside = (block_near >= 0).reshape(-1)
            neighbour_data = jnp.where(inside, local_data, arrived).reshape(9, FACE_BASIS, 4, E_DEV)
            own_data = own_faces.reshape(9, FACE_BASIS, 4, E_DEV)
            return face_update(block_state, block_volume, own_data, neighbour_data, block_orient, block_normals, values, wave_speed, rotate, face_lift)
        current = lax.map(block_update, (block_ids, current, volume, mat_blocks, normal_blocks, orient_blocks, near_blocks, near_face_blocks, recv_all))
    return jnp.moveaxis(current, 0, -2).reshape(dof_values.shape)
```

```python
import jax
import jax.numpy as jnp
from jax import lax
from jax.sharding import PartitionSpec as P

ORDER = 6
STEPS = 2


exact_mode = lax.Precision.HIGHEST
time_step = 0.8
OFFSETS = ((-1, -1), (-1, 0), (-1, 1), (0, -1), (0, 1), (1, -1), (1, 0), (1, 1))
ENTRIES = (
    (0, 0, 6, 0),
    (0, 1, 6, 1),
    (0, 2, 6, 1),
    (0, 3, 7, 2),
    (0, 5, 8, 2),
    (0, 6, 0, 3),
    (0, 7, 3, 3),
    (0, 8, 5, 3),
    (1, 0, 7, 1),
    (1, 1, 7, 0),
    (1, 2, 7, 1),
    (1, 3, 6, 2),
    (1, 4, 8, 2),
    (1, 6, 3, 3),
    (1, 7, 1, 3),
    (1, 8, 4, 3),
    (2, 0, 8, 1),
    (2, 1, 8, 1),
    (2, 2, 8, 0),
    (2, 4, 7, 2),
    (2, 5, 6, 2),
    (2, 6, 5, 3),
    (2, 7, 4, 3),
    (2, 8, 2, 3),
)


def shifted(x, axis, by):
    devices = lax.axis_size(axis)
    pairs = [(i, i + by) for i in range(devices) if 0 <= i + by < devices]
    return lax.ppermute(x, axis, pairs)


def element_params(material, material_id, normals):
    id_range = jnp.arange(material.shape[0], dtype=jnp.int32)
    onehot = (material_id[None, :] == id_range[:, None]).astype(material.dtype)
    params = jnp.dot(material.T, onehot, precision=exact_mode)
    density, lame_first, shear_modulus = (params[0], params[1], params[2])
    values = (-(lame_first + 2.0 * shear_modulus), -lame_first, -shear_modulus, -1.0 / density)
    wave_speed = jnp.sqrt((lame_first + 2.0 * shear_modulus) / density) * jnp.sum(
        jnp.abs(normals), axis=1
    )
    return (values, wave_speed)


def elastic_apply(parts, values):
    result = [None] * 9
    for comp_axis, row_index, col_index, kind_index in ENTRIES:
        term = values[kind_index] * parts[comp_axis][col_index]
        result[row_index] = term if result[row_index] is None else result[row_index] + term
    return jnp.stack(result, axis=0)


def star_apply(slopes, inv_jacobian, values):
    parts = [jnp.sum(inv_jacobian[:, k][:, None, None, :] * slopes, axis=0) for k in range(3)]
    return elastic_apply(parts, values)


def predict(current, inv_jacobian, values, grad_matrix):
    derivative = current
    integrated = time_step * current
    factor = time_step
    for power_level in range(1, ORDER):
        slopes = jnp.einsum("dab,qbe->dqae", grad_matrix, derivative, precision=exact_mode)
        derivative = -star_apply(slopes, inv_jacobian, values)
        factor = factor * time_step / (power_level + 1)
        integrated = integrated + factor * derivative
    return integrated


def local_part(current, inv_jacobian, values, grad_matrix, stiff_matrix, face_proj):
    integrated = predict(current, inv_jacobian, values, grad_matrix)
    slopes = jnp.einsum("dab,qbe->dqae", stiff_matrix, integrated, precision=exact_mode)
    volume = star_apply(slopes, inv_jacobian, values)
    face_data = jnp.einsum("fib,qbe->qife", face_proj, integrated, precision=exact_mode)
    return (volume, face_data)


def face_update(
    current,
    volume,
    face_data,
    neighbour_data,
    orientation,
    normals,
    values,
    wave_speed,
    rotate,
    face_lift,
):
    turned = jnp.einsum("hil,qlfe->hqife", rotate, neighbour_data, precision=exact_mode)
    chosen = (orientation[None] == jnp.arange(3, dtype=jnp.int32)[:, None, None]).astype(
        current.dtype
    )
    turned = jnp.sum(turned * chosen[:, None, None, :, :], axis=0)
    both = face_data + turned
    apart = face_data - turned
    parts = [normals[:, k, :][None, None] * both for k in range(3)]
    flux_total = 0.5 * (elastic_apply(parts, values) + wave_speed[None, None] * apart)
    lifted = jnp.einsum("fai,pife->pae", face_lift, flux_total, precision=exact_mode)
    return current + volume - lifted


def deliver(outgoing):
    rows = lax.axis_size("prow")
    cols = lax.axis_size("pcol")
    pieces = [None] * 8
    for direction, (row_step, col_step) in enumerate(OFFSETS):
        pairs = [
            (r * cols + c, (r + row_step) * cols + (c + col_step))
            for r in range(rows)
            for c in range(cols)
            if 0 <= r + row_step < rows and 0 <= c + col_step < cols
        ]
        pieces[7 - direction] = lax.ppermute(outgoing[:, direction], ("prow", "pcol"), pairs)
    return jnp.stack(pieces, axis=1)


def per_device(
    dof_values,
    grad_matrix,
    stiff_matrix,
    face_proj,
    face_lift,
    rotate,
    material,
    material_id,
    inv_jacobian,
    normals,
    orientation,
    neighbour,
    neighbour_face,
    send_list,
    recv_list,
):
    elem_count = dof_values.shape[2]
    face_width = face_proj.shape[1]
    face_total = 4 * elem_count
    dtype = dof_values.dtype
    values, wave_speed = element_params(material, material_id, normals)
    face_ids = jnp.arange(face_total, dtype=jnp.int32)
    inside = (neighbour >= 0).reshape(-1)
    local_index = (neighbour_face * elem_count + jnp.maximum(neighbour, 0)).reshape(-1)
    gather_local = ((local_index[None, :] == face_ids[:, None]) & inside[None, :]).astype(dtype)
    source_ids = send_list[0, 0]
    slot_total = source_ids.shape[1]
    gather_out = (source_ids.reshape(-1)[None, :] == face_ids[:, None]).astype(dtype)
    targets = recv_list[0, 0].reshape(-1)
    scatter_in = ((targets[:, None] == face_ids[None, :]) & ~inside[None, :]).astype(dtype)
    current = dof_values
    for time_index in range(STEPS):
        volume, face_data = local_part(
            current, inv_jacobian, values, grad_matrix, stiff_matrix, face_proj
        )
        flat_faces = face_data.reshape(9 * face_width, face_total)
        outgoing = jnp.dot(flat_faces, gather_out, precision=exact_mode).reshape(
            9 * face_width, 8, slot_total
        )
        received = deliver(outgoing).reshape(9 * face_width, 8 * slot_total)
        neighbour_data = jnp.dot(flat_faces, gather_local, precision=exact_mode) + jnp.dot(
            received, scatter_in, precision=exact_mode
        )
        neighbour_data = neighbour_data.reshape(9, face_width, 4, elem_count)
        current = face_update(
            current,
            volume,
            face_data,
            neighbour_data,
            orientation,
            normals,
            values,
            wave_speed,
            rotate,
            face_lift,
        )
    return current


def solution(mesh):
    return jax.shard_map(
        per_device,
        mesh=mesh,
        in_specs=(
            P(None, None, ("prow", "pcol")),
            P(),
            P(),
            P(),
            P(),
            P(),
            P(),
            P(("prow", "pcol")),
            P(None, None, ("prow", "pcol")),
            P(None, None, ("prow", "pcol")),
            P(None, ("prow", "pcol")),
            P(None, ("prow", "pcol")),
            P(None, ("prow", "pcol")),
            P("prow", "pcol", None, None),
            P("prow", "pcol", None, None),
        ),
        out_specs=P(None, None, ("prow", "pcol")),
        check_vma=False,
    )
```

```python
import jax
import jax.numpy as jnp
from jax import lax
from jax.sharding import PartitionSpec as P

ORDER = 6
STEPS = 2


exact_mode = lax.Precision.HIGHEST
time_step = 0.8
OFFSETS = ((-1, -1), (-1, 0), (-1, 1), (0, -1), (0, 1), (1, -1), (1, 0), (1, 1))
ENTRIES = (
    (0, 0, 6, 0),
    (0, 1, 6, 1),
    (0, 2, 6, 1),
    (0, 3, 7, 2),
    (0, 5, 8, 2),
    (0, 6, 0, 3),
    (0, 7, 3, 3),
    (0, 8, 5, 3),
    (1, 0, 7, 1),
    (1, 1, 7, 0),
    (1, 2, 7, 1),
    (1, 3, 6, 2),
    (1, 4, 8, 2),
    (1, 6, 3, 3),
    (1, 7, 1, 3),
    (1, 8, 4, 3),
    (2, 0, 8, 1),
    (2, 1, 8, 1),
    (2, 2, 8, 0),
    (2, 4, 7, 2),
    (2, 5, 6, 2),
    (2, 6, 5, 3),
    (2, 7, 4, 3),
    (2, 8, 2, 3),
)


def shifted(x, axis, by):
    devices = lax.axis_size(axis)
    pairs = [(i, i + by) for i in range(devices) if 0 <= i + by < devices]
    return lax.ppermute(x, axis, pairs)


def element_params(material, material_id, normals):
    id_range = jnp.arange(material.shape[0], dtype=jnp.int32)
    onehot = (material_id[None, :] == id_range[:, None]).astype(material.dtype)
    params = jnp.dot(material.T, onehot, precision=exact_mode)
    density, lame_first, shear_modulus = (params[0], params[1], params[2])
    values = (-(lame_first + 2.0 * shear_modulus), -lame_first, -shear_modulus, -1.0 / density)
    wave_speed = jnp.sqrt((lame_first + 2.0 * shear_modulus) / density) * jnp.sum(
        jnp.abs(normals), axis=1
    )
    return (values, wave_speed)


def elastic_apply(parts, values):
    result = [None] * 9
    for comp_axis, row_index, col_index, kind_index in ENTRIES:
        term = values[kind_index] * parts[comp_axis][col_index]
        result[row_index] = term if result[row_index] is None else result[row_index] + term
    return jnp.stack(result, axis=0)


def star_apply(slopes, inv_jacobian, values):
    parts = [jnp.sum(inv_jacobian[:, k][:, None, None, :] * slopes, axis=0) for k in range(3)]
    return elastic_apply(parts, values)


def predict(current, inv_jacobian, values, grad_matrix):
    derivative = current
    integrated = time_step * current
    factor = time_step
    for power_level in range(1, ORDER):
        slopes = jnp.einsum("dab,qbe->dqae", grad_matrix, derivative, precision=exact_mode)
        derivative = -star_apply(slopes, inv_jacobian, values)
        factor = factor * time_step / (power_level + 1)
        integrated = integrated + factor * derivative
    return integrated


def local_part(current, inv_jacobian, values, grad_matrix, stiff_matrix, face_proj):
    integrated = predict(current, inv_jacobian, values, grad_matrix)
    slopes = jnp.einsum("dab,qbe->dqae", stiff_matrix, integrated, precision=exact_mode)
    volume = star_apply(slopes, inv_jacobian, values)
    face_data = jnp.einsum("fib,qbe->qife", face_proj, integrated, precision=exact_mode)
    return (volume, face_data)


def face_update(
    current,
    volume,
    face_data,
    neighbour_data,
    orientation,
    normals,
    values,
    wave_speed,
    rotate,
    face_lift,
):
    turned = jnp.einsum("hil,qlfe->hqife", rotate, neighbour_data, precision=exact_mode)
    chosen = (orientation[None] == jnp.arange(3, dtype=jnp.int32)[:, None, None]).astype(
        current.dtype
    )
    turned = jnp.sum(turned * chosen[:, None, None, :, :], axis=0)
    both = face_data + turned
    apart = face_data - turned
    parts = [normals[:, k, :][None, None] * both for k in range(3)]
    flux_total = 0.5 * (elastic_apply(parts, values) + wave_speed[None, None] * apart)
    lifted = jnp.einsum("fai,pife->pae", face_lift, flux_total, precision=exact_mode)
    return current + volume - lifted


SEND_ORDER = (0, 3, 5, 2, 4, 7, 1, 6)
RECV_ORDER = (4, 3, 6, 5, 7, 1, 0, 2)


def deliver(outgoing, slot_total):
    group = 3 * slot_total
    left = shifted(outgoing[:group], "pcol", -1)
    right = shifted(outgoing[group : 2 * group], "pcol", 1)
    up_bundle = jnp.concatenate(
        [outgoing[2 * group : 2 * group + slot_total], right[:slot_total], left[:slot_total]], axis=0
    )
    down_bundle = jnp.concatenate(
        [outgoing[2 * group + slot_total :], right[2 * slot_total :], left[2 * slot_total :]], axis=0
    )
    up = shifted(up_bundle, "prow", -1)
    down = shifted(down_bundle, "prow", 1)
    return jnp.concatenate(
        [left[slot_total : 2 * slot_total], right[slot_total : 2 * slot_total], up, down], axis=0
    )


def per_device(
    dof_values,
    grad_matrix,
    stiff_matrix,
    face_proj,
    face_lift,
    rotate,
    material,
    material_id,
    inv_jacobian,
    normals,
    orientation,
    neighbour,
    neighbour_face,
    send_list,
    recv_list,
):
    elem_count = dof_values.shape[2]
    face_width = face_proj.shape[1]
    face_total = 4 * elem_count
    dtype = dof_values.dtype
    values, wave_speed = element_params(material, material_id, normals)
    face_ids = jnp.arange(face_total, dtype=jnp.int32)
    inside = (neighbour >= 0).reshape(-1)
    local_index = (neighbour_face * elem_count + jnp.maximum(neighbour, 0)).reshape(-1)
    gather_local = ((local_index[None, :] == face_ids[:, None]) & inside[None, :]).astype(dtype)
    source_ids = send_list[0, 0][jnp.array(SEND_ORDER)]
    slot_total = source_ids.shape[1]
    gather_out = (source_ids.reshape(-1)[:, None] == face_ids[None, :]).astype(dtype)
    targets = recv_list[0, 0][jnp.array(RECV_ORDER)].reshape(-1)
    scatter_in = ((targets[:, None] == face_ids[None, :]) & ~inside[None, :]).astype(dtype)
    current = dof_values
    for time_index in range(STEPS):
        volume, face_data = local_part(
            current, inv_jacobian, values, grad_matrix, stiff_matrix, face_proj
        )
        flat_faces = face_data.reshape(9 * face_width, face_total)
        outgoing = lax.dot_general(
            gather_out, flat_faces, (((1,), (1,)), ((), ())), precision=exact_mode
        )
        received = deliver(outgoing, slot_total)
        neighbour_data = jnp.dot(flat_faces, gather_local, precision=exact_mode) + lax.dot_general(
            received, scatter_in, (((0,), (0,)), ((), ())), precision=exact_mode
        )
        neighbour_data = neighbour_data.reshape(9, face_width, 4, elem_count)
        current = face_update(
            current,
            volume,
            face_data,
            neighbour_data,
            orientation,
            normals,
            values,
            wave_speed,
            rotate,
            face_lift,
        )
    return current


def solution(mesh):
    return jax.shard_map(
        per_device,
        mesh=mesh,
        in_specs=(
            P(None, None, ("prow", "pcol")),
            P(),
            P(),
            P(),
            P(),
            P(),
            P(),
            P(("prow", "pcol")),
            P(None, None, ("prow", "pcol")),
            P(None, None, ("prow", "pcol")),
            P(None, ("prow", "pcol")),
            P(None, ("prow", "pcol")),
            P(None, ("prow", "pcol")),
            P("prow", "pcol", None, None),
            P("prow", "pcol", None, None),
        ),
        out_specs=P(None, None, ("prow", "pcol")),
        check_vma=False,
    )
```

```python
import jax
import jax.numpy as jnp
from jax import lax
from jax.sharding import PartitionSpec as P

ORDER = 6
STEPS = 2


exact_mode = lax.Precision.HIGHEST
fast_mode = lax.Precision.HIGH
time_step = 0.8
OFFSETS = ((-1, -1), (-1, 0), (-1, 1), (0, -1), (0, 1), (1, -1), (1, 0), (1, 1))
ENTRIES = (
    (0, 0, 6, 0),
    (0, 1, 6, 1),
    (0, 2, 6, 1),
    (0, 3, 7, 2),
    (0, 5, 8, 2),
    (0, 6, 0, 3),
    (0, 7, 3, 3),
    (0, 8, 5, 3),
    (1, 0, 7, 1),
    (1, 1, 7, 0),
    (1, 2, 7, 1),
    (1, 3, 6, 2),
    (1, 4, 8, 2),
    (1, 6, 3, 3),
    (1, 7, 1, 3),
    (1, 8, 4, 3),
    (2, 0, 8, 1),
    (2, 1, 8, 1),
    (2, 2, 8, 0),
    (2, 4, 7, 2),
    (2, 5, 6, 2),
    (2, 6, 5, 3),
    (2, 7, 4, 3),
    (2, 8, 2, 3),
)


def shifted(x, axis, by):
    devices = lax.axis_size(axis)
    pairs = [(i, i + by) for i in range(devices) if 0 <= i + by < devices]
    return lax.ppermute(x, axis, pairs)


def element_params(material, material_id, normals):
    id_range = jnp.arange(material.shape[0], dtype=jnp.int32)
    onehot = (material_id[None, :] == id_range[:, None]).astype(material.dtype)
    params = jnp.dot(material.T, onehot, precision=exact_mode)
    density, lame_first, shear_modulus = (params[0], params[1], params[2])
    values = (-(lame_first + 2.0 * shear_modulus), -lame_first, -shear_modulus, -1.0 / density)
    wave_speed = jnp.sqrt((lame_first + 2.0 * shear_modulus) / density) * jnp.sum(
        jnp.abs(normals), axis=1
    )
    return (values, wave_speed)


def elastic_apply(parts, values):
    result = [None] * 9
    for comp_axis, row_index, col_index, kind_index in ENTRIES:
        term = values[kind_index] * parts[comp_axis][col_index]
        result[row_index] = term if result[row_index] is None else result[row_index] + term
    return jnp.stack(result, axis=0)


def star_apply(slopes, inv_jacobian, values):
    parts = [jnp.sum(inv_jacobian[:, k][:, None, None, :] * slopes, axis=0) for k in range(3)]
    return elastic_apply(parts, values)


def predict(current, inv_jacobian, values, grad_matrix):
    derivative = current
    integrated = time_step * current
    factor = time_step
    for power_level in range(1, ORDER):
        slopes = jnp.einsum("dab,qbe->dqae", grad_matrix, derivative, precision=fast_mode)
        derivative = -star_apply(slopes, inv_jacobian, values)
        factor = factor * time_step / (power_level + 1)
        integrated = integrated + factor * derivative
    return integrated


def local_part(current, inv_jacobian, values, grad_matrix, stiff_matrix, face_proj):
    integrated = predict(current, inv_jacobian, values, grad_matrix)
    slopes = jnp.einsum("dab,qbe->dqae", stiff_matrix, integrated, precision=fast_mode)
    volume = star_apply(slopes, inv_jacobian, values)
    face_data = jnp.einsum("fib,qbe->qife", face_proj, integrated, precision=fast_mode)
    return (volume, face_data)


def face_update(
    current,
    volume,
    face_data,
    neighbour_data,
    orientation,
    normals,
    values,
    wave_speed,
    rotate,
    face_lift,
):
    turned = jnp.einsum("hil,qlfe->hqife", rotate, neighbour_data, precision=fast_mode)
    chosen = (orientation[None] == jnp.arange(3, dtype=jnp.int32)[:, None, None]).astype(
        current.dtype
    )
    turned = jnp.sum(turned * chosen[:, None, None, :, :], axis=0)
    both = face_data + turned
    apart = face_data - turned
    parts = [normals[:, k, :][None, None] * both for k in range(3)]
    flux_total = 0.5 * (elastic_apply(parts, values) + wave_speed[None, None] * apart)
    lifted = jnp.einsum("fai,pife->pae", face_lift, flux_total, precision=fast_mode)
    return current + volume - lifted


SEND_ORDER = (0, 3, 5, 2, 4, 7, 1, 6)
RECV_ORDER = (4, 3, 6, 5, 7, 1, 0, 2)


def deliver(outgoing, slot_total):
    group = 3 * slot_total
    left = shifted(outgoing[:group], "pcol", -1)
    right = shifted(outgoing[group : 2 * group], "pcol", 1)
    up_bundle = jnp.concatenate(
        [outgoing[2 * group : 2 * group + slot_total], right[:slot_total], left[:slot_total]], axis=0
    )
    down_bundle = jnp.concatenate(
        [outgoing[2 * group + slot_total :], right[2 * slot_total :], left[2 * slot_total :]], axis=0
    )
    up = shifted(up_bundle, "prow", -1)
    down = shifted(down_bundle, "prow", 1)
    return jnp.concatenate(
        [left[slot_total : 2 * slot_total], right[slot_total : 2 * slot_total], up, down], axis=0
    )


def per_device(
    dof_values,
    grad_matrix,
    stiff_matrix,
    face_proj,
    face_lift,
    rotate,
    material,
    material_id,
    inv_jacobian,
    normals,
    orientation,
    neighbour,
    neighbour_face,
    send_list,
    recv_list,
):
    elem_count = dof_values.shape[2]
    face_width = face_proj.shape[1]
    face_total = 4 * elem_count
    dtype = dof_values.dtype
    values, wave_speed = element_params(material, material_id, normals)
    face_ids = jnp.arange(face_total, dtype=jnp.int32)
    inside = (neighbour >= 0).reshape(-1)
    local_index = (neighbour_face * elem_count + jnp.maximum(neighbour, 0)).reshape(-1)
    gather_local = ((local_index[None, :] == face_ids[:, None]) & inside[None, :]).astype(dtype)
    source_ids = send_list[0, 0][jnp.array(SEND_ORDER)]
    slot_total = source_ids.shape[1]
    gather_out = (source_ids.reshape(-1)[:, None] == face_ids[None, :]).astype(dtype)
    targets = recv_list[0, 0][jnp.array(RECV_ORDER)].reshape(-1)
    scatter_in = ((targets[:, None] == face_ids[None, :]) & ~inside[None, :]).astype(dtype)
    current = dof_values
    for time_index in range(STEPS):
        volume, face_data = local_part(
            current, inv_jacobian, values, grad_matrix, stiff_matrix, face_proj
        )
        flat_faces = face_data.reshape(9 * face_width, face_total)
        outgoing = lax.dot_general(
            gather_out, flat_faces, (((1,), (1,)), ((), ())), precision=exact_mode
        )
        received = deliver(outgoing, slot_total)
        neighbour_data = jnp.dot(flat_faces, gather_local, precision=exact_mode) + lax.dot_general(
            received, scatter_in, (((0,), (0,)), ((), ())), precision=exact_mode
        )
        neighbour_data = neighbour_data.reshape(9, face_width, 4, elem_count)
        current = face_update(
            current,
            volume,
            face_data,
            neighbour_data,
            orientation,
            normals,
            values,
            wave_speed,
            rotate,
            face_lift,
        )
    return current


def solution(mesh):
    return jax.shard_map(
        per_device,
        mesh=mesh,
        in_specs=(
            P(None, None, ("prow", "pcol")),
            P(),
            P(),
            P(),
            P(),
            P(),
            P(),
            P(("prow", "pcol")),
            P(None, None, ("prow", "pcol")),
            P(None, None, ("prow", "pcol")),
            P(None, ("prow", "pcol")),
            P(None, ("prow", "pcol")),
            P(None, ("prow", "pcol")),
            P("prow", "pcol", None, None),
            P("prow", "pcol", None, None),
        ),
        out_specs=P(None, None, ("prow", "pcol")),
        check_vma=False,
    )
```

```python
import jax
import jax.numpy as jnp
from jax import lax
from jax.sharding import PartitionSpec as P

ORDER = 6
STEPS = 2


exact_mode = lax.Precision.HIGHEST
fast_mode = lax.Precision.HIGH
time_step = 0.8
OFFSETS = ((-1, -1), (-1, 0), (-1, 1), (0, -1), (0, 1), (1, -1), (1, 0), (1, 1))
ENTRIES = (
    (0, 0, 6, 0),
    (0, 1, 6, 1),
    (0, 2, 6, 1),
    (0, 3, 7, 2),
    (0, 5, 8, 2),
    (0, 6, 0, 3),
    (0, 7, 3, 3),
    (0, 8, 5, 3),
    (1, 0, 7, 1),
    (1, 1, 7, 0),
    (1, 2, 7, 1),
    (1, 3, 6, 2),
    (1, 4, 8, 2),
    (1, 6, 3, 3),
    (1, 7, 1, 3),
    (1, 8, 4, 3),
    (2, 0, 8, 1),
    (2, 1, 8, 1),
    (2, 2, 8, 0),
    (2, 4, 7, 2),
    (2, 5, 6, 2),
    (2, 6, 5, 3),
    (2, 7, 4, 3),
    (2, 8, 2, 3),
)


def shifted(x, axis, by):
    devices = lax.axis_size(axis)
    pairs = [(i, i + by) for i in range(devices) if 0 <= i + by < devices]
    return lax.ppermute(x, axis, pairs)


def element_params(material, material_id, normals):
    id_range = jnp.arange(material.shape[0], dtype=jnp.int32)
    chosen = material_id[None, None, :] == id_range[:, None, None]
    params = jnp.sum(jnp.where(chosen, material[:, :, None], 0.0), axis=0)
    density, lame_first, shear_modulus = (params[0], params[1], params[2])
    values = (-(lame_first + 2.0 * shear_modulus), -lame_first, -shear_modulus, -1.0 / density)
    wave_speed = jnp.sqrt((lame_first + 2.0 * shear_modulus) / density) * jnp.sum(
        jnp.abs(normals), axis=1
    )
    return (values, wave_speed)


def elastic_apply(parts, values):
    result = [None] * 9
    for comp_axis, row_index, col_index, kind_index in ENTRIES:
        term = values[kind_index] * parts[comp_axis][col_index]
        result[row_index] = term if result[row_index] is None else result[row_index] + term
    return jnp.stack(result, axis=0)


def star_apply(slopes, inv_jacobian, values):
    parts = [jnp.sum(inv_jacobian[:, k][:, None, None, :] * slopes, axis=0) for k in range(3)]
    return elastic_apply(parts, values)


def predict(current, inv_jacobian, values, grad_matrix):
    derivative = current
    integrated = time_step * current
    factor = time_step
    for power_level in range(1, ORDER):
        slopes = jnp.einsum("dab,qbe->dqae", grad_matrix, derivative, precision=fast_mode)
        derivative = -star_apply(slopes, inv_jacobian, values)
        factor = factor * time_step / (power_level + 1)
        integrated = integrated + factor * derivative
    return integrated


def local_part(current, inv_jacobian, values, grad_matrix, stiff_matrix, face_proj):
    integrated = predict(current, inv_jacobian, values, grad_matrix)
    slopes = jnp.einsum("dab,qbe->dqae", stiff_matrix, integrated, precision=fast_mode)
    volume = star_apply(slopes, inv_jacobian, values)
    face_data = jnp.einsum("fib,qbe->qife", face_proj, integrated, precision=fast_mode)
    return (volume, face_data)


def face_update(
    current,
    volume,
    face_data,
    neighbour_data,
    orientation,
    normals,
    values,
    wave_speed,
    rotate,
    face_lift,
):
    turned = jnp.einsum("hil,qlfe->hqife", rotate, neighbour_data, precision=fast_mode)
    chosen = (orientation[None] == jnp.arange(3, dtype=jnp.int32)[:, None, None]).astype(
        current.dtype
    )
    turned = jnp.sum(turned * chosen[:, None, None, :, :], axis=0)
    both = face_data + turned
    apart = face_data - turned
    parts = [normals[:, k, :][None, None] * both for k in range(3)]
    flux_total = 0.5 * (elastic_apply(parts, values) + wave_speed[None, None] * apart)
    lifted = jnp.einsum("fai,pife->pae", face_lift, flux_total, precision=fast_mode)
    return current + volume - lifted


SEND_ORDER = (0, 3, 5, 2, 4, 7, 1, 6)
RECV_ORDER = (4, 3, 6, 5, 7, 1, 0, 2)


def deliver(outgoing, slot_total):
    group = 3 * slot_total
    left = shifted(outgoing[:group], "pcol", -1)
    right = shifted(outgoing[group : 2 * group], "pcol", 1)
    up_bundle = jnp.concatenate(
        [outgoing[2 * group : 2 * group + slot_total], right[:slot_total], left[:slot_total]], axis=0
    )
    down_bundle = jnp.concatenate(
        [outgoing[2 * group + slot_total :], right[2 * slot_total :], left[2 * slot_total :]], axis=0
    )
    up = shifted(up_bundle, "prow", -1)
    down = shifted(down_bundle, "prow", 1)
    return jnp.concatenate(
        [left[slot_total : 2 * slot_total], right[slot_total : 2 * slot_total], up, down], axis=0
    )


def per_device(
    dof_values,
    grad_matrix,
    stiff_matrix,
    face_proj,
    face_lift,
    rotate,
    material,
    material_id,
    inv_jacobian,
    normals,
    orientation,
    neighbour,
    neighbour_face,
    send_list,
    recv_list,
):
    elem_count = dof_values.shape[2]
    face_width = face_proj.shape[1]
    face_total = 4 * elem_count
    dtype = dof_values.dtype
    values, wave_speed = element_params(material, material_id, normals)
    face_ids = jnp.arange(face_total, dtype=jnp.int32)
    inside = (neighbour >= 0).reshape(-1)
    local_index = (neighbour_face * elem_count + jnp.maximum(neighbour, 0)).reshape(-1)
    gather_local = ((local_index[None, :] == face_ids[:, None]) & inside[None, :]).astype(dtype)
    source_ids = jnp.concatenate([send_list[0, 0, d : d + 1] for d in SEND_ORDER], axis=0)
    slot_total = source_ids.shape[1]
    gather_out = (source_ids.reshape(-1)[:, None] == face_ids[None, :]).astype(dtype)
    targets = jnp.concatenate([recv_list[0, 0, d] for d in RECV_ORDER], axis=0)
    scatter_in = ((targets[:, None] == face_ids[None, :]) & ~inside[None, :]).astype(dtype)
    current = dof_values
    for time_index in range(STEPS):
        volume, face_data = local_part(
            current, inv_jacobian, values, grad_matrix, stiff_matrix, face_proj
        )
        flat_faces = face_data.reshape(9 * face_width, face_total)
        outgoing = lax.dot_general(
            gather_out, flat_faces, (((1,), (1,)), ((), ())), precision=exact_mode
        )
        received = deliver(outgoing, slot_total)
        neighbour_data = jnp.dot(flat_faces, gather_local, precision=exact_mode) + lax.dot_general(
            received, scatter_in, (((0,), (0,)), ((), ())), precision=exact_mode
        )
        neighbour_data = neighbour_data.reshape(9, face_width, 4, elem_count)
        current = face_update(
            current,
            volume,
            face_data,
            neighbour_data,
            orientation,
            normals,
            values,
            wave_speed,
            rotate,
            face_lift,
        )
    return current


def solution(mesh):
    return jax.shard_map(
        per_device,
        mesh=mesh,
        in_specs=(
            P(None, None, ("prow", "pcol")),
            P(),
            P(),
            P(),
            P(),
            P(),
            P(),
            P(("prow", "pcol")),
            P(None, None, ("prow", "pcol")),
            P(None, None, ("prow", "pcol")),
            P(None, ("prow", "pcol")),
            P(None, ("prow", "pcol")),
            P(None, ("prow", "pcol")),
            P("prow", "pcol", None, None),
            P("prow", "pcol", None, None),
        ),
        out_specs=P(None, None, ("prow", "pcol")),
        check_vma=False,
    )
```

```python
import jax
import jax.numpy as jnp
from jax import lax
from jax.sharding import PartitionSpec as P

ORDER = 6
STEPS = 2


exact_mode = lax.Precision.HIGHEST
fast_mode = lax.Precision.HIGH
time_step = 0.8
OFFSETS = ((-1, -1), (-1, 0), (-1, 1), (0, -1), (0, 1), (1, -1), (1, 0), (1, 1))
ENTRIES = (
    (0, 0, 6, 0),
    (0, 1, 6, 1),
    (0, 2, 6, 1),
    (0, 3, 7, 2),
    (0, 5, 8, 2),
    (0, 6, 0, 3),
    (0, 7, 3, 3),
    (0, 8, 5, 3),
    (1, 0, 7, 1),
    (1, 1, 7, 0),
    (1, 2, 7, 1),
    (1, 3, 6, 2),
    (1, 4, 8, 2),
    (1, 6, 3, 3),
    (1, 7, 1, 3),
    (1, 8, 4, 3),
    (2, 0, 8, 1),
    (2, 1, 8, 1),
    (2, 2, 8, 0),
    (2, 4, 7, 2),
    (2, 5, 6, 2),
    (2, 6, 5, 3),
    (2, 7, 4, 3),
    (2, 8, 2, 3),
)


def shifted(x, axis, by):
    devices = lax.axis_size(axis)
    pairs = [(i, i + by) for i in range(devices) if 0 <= i + by < devices]
    return lax.ppermute(x, axis, pairs)


def element_params(material, material_id, normals):
    id_range = jnp.arange(material.shape[0], dtype=jnp.int32)
    chosen = material_id[None, None, :] == id_range[:, None, None]
    params = jnp.sum(jnp.where(chosen, material[:, :, None], 0.0), axis=0)
    density, lame_first, shear_modulus = (params[0], params[1], params[2])
    values = (-(lame_first + 2.0 * shear_modulus), -lame_first, -shear_modulus, -1.0 / density)
    wave_speed = jnp.sqrt((lame_first + 2.0 * shear_modulus) / density) * jnp.sum(
        jnp.abs(normals), axis=1
    )
    return (values, wave_speed)


def elastic_apply(parts, values):
    result = [None] * 9
    for comp_axis, row_index, col_index, kind_index in ENTRIES:
        term = values[kind_index] * parts[comp_axis][col_index]
        result[row_index] = term if result[row_index] is None else result[row_index] + term
    return jnp.stack(result, axis=0)


def star_coefficients(inv_jacobian, values):
    return {
        (d, row_index, col_index): inv_jacobian[d, comp_axis] * values[kind_index]
        for d in range(3)
        for comp_axis, row_index, col_index, kind_index in ENTRIES
    }


def star_apply(slopes, coefficients):
    result = [None] * 9
    for (d, row_index, col_index), coefficient in coefficients.items():
        term = coefficient[None, :] * slopes[d, col_index]
        result[row_index] = term if result[row_index] is None else result[row_index] + term
    return jnp.stack(result, axis=0)


def predict(current, coefficients, grad_matrix):
    derivative = current
    integrated = time_step * current
    factor = time_step
    for power_level in range(1, ORDER):
        slopes = jnp.einsum("dab,qbe->dqae", grad_matrix, derivative, precision=fast_mode)
        derivative = -star_apply(slopes, coefficients)
        factor = factor * time_step / (power_level + 1)
        integrated = integrated + factor * derivative
    return integrated


def local_part(current, coefficients, grad_matrix, stiff_matrix, face_proj):
    integrated = predict(current, coefficients, grad_matrix)
    slopes = jnp.einsum("dab,qbe->dqae", stiff_matrix, integrated, precision=fast_mode)
    volume = star_apply(slopes, coefficients)
    face_data = jnp.einsum("fib,qbe->qife", face_proj, integrated, precision=fast_mode)
    return (volume, face_data)


def face_update(
    current,
    volume,
    face_data,
    neighbour_data,
    orientation,
    normals,
    values,
    wave_speed,
    rotate,
    face_lift,
):
    turned = jnp.einsum("hil,qlfe->hqife", rotate, neighbour_data, precision=fast_mode)
    chosen = (orientation[None] == jnp.arange(3, dtype=jnp.int32)[:, None, None]).astype(
        current.dtype
    )
    turned = jnp.sum(turned * chosen[:, None, None, :, :], axis=0)
    both = face_data + turned
    apart = face_data - turned
    parts = [normals[:, k, :][None, None] * both for k in range(3)]
    flux_total = 0.5 * (elastic_apply(parts, values) + wave_speed[None, None] * apart)
    lifted = jnp.einsum("fai,pife->pae", face_lift, flux_total, precision=fast_mode)
    return current + volume - lifted


SEND_ORDER = (0, 3, 5, 2, 4, 7, 1, 6)
RECV_ORDER = (4, 3, 6, 5, 7, 1, 0, 2)


def deliver(outgoing, slot_total):
    group = 3 * slot_total
    left = shifted(outgoing[:group], "pcol", -1)
    right = shifted(outgoing[group : 2 * group], "pcol", 1)
    up_bundle = jnp.concatenate(
        [outgoing[2 * group : 2 * group + slot_total], right[:slot_total], left[:slot_total]], axis=0
    )
    down_bundle = jnp.concatenate(
        [outgoing[2 * group + slot_total :], right[2 * slot_total :], left[2 * slot_total :]], axis=0
    )
    up = shifted(up_bundle, "prow", -1)
    down = shifted(down_bundle, "prow", 1)
    return jnp.concatenate(
        [left[slot_total : 2 * slot_total], right[slot_total : 2 * slot_total], up, down], axis=0
    )


def per_device(
    dof_values,
    grad_matrix,
    stiff_matrix,
    face_proj,
    face_lift,
    rotate,
    material,
    material_id,
    inv_jacobian,
    normals,
    orientation,
    neighbour,
    neighbour_face,
    send_list,
    recv_list,
):
    elem_count = dof_values.shape[2]
    face_width = face_proj.shape[1]
    face_total = 4 * elem_count
    dtype = dof_values.dtype
    values, wave_speed = element_params(material, material_id, normals)
    coefficients = star_coefficients(inv_jacobian, values)
    face_ids = jnp.arange(face_total, dtype=jnp.int32)
    inside = (neighbour >= 0).reshape(-1)
    local_index = (neighbour_face * elem_count + jnp.maximum(neighbour, 0)).reshape(-1)
    gather_local = ((local_index[None, :] == face_ids[:, None]) & inside[None, :]).astype(dtype)
    source_ids = jnp.concatenate([send_list[0, 0, d : d + 1] for d in SEND_ORDER], axis=0)
    slot_total = source_ids.shape[1]
    gather_out = (source_ids.reshape(-1)[:, None] == face_ids[None, :]).astype(dtype)
    targets = jnp.concatenate([recv_list[0, 0, d] for d in RECV_ORDER], axis=0)
    scatter_in = ((targets[:, None] == face_ids[None, :]) & ~inside[None, :]).astype(dtype)
    current = dof_values
    for time_index in range(STEPS):
        volume, face_data = local_part(
            current, coefficients, grad_matrix, stiff_matrix, face_proj
        )
        flat_faces = face_data.reshape(9 * face_width, face_total)
        outgoing = lax.dot_general(
            gather_out, flat_faces, (((1,), (1,)), ((), ())), precision=exact_mode
        )
        received = deliver(outgoing, slot_total)
        neighbour_data = jnp.dot(flat_faces, gather_local, precision=exact_mode) + lax.dot_general(
            received, scatter_in, (((0,), (0,)), ((), ())), precision=exact_mode
        )
        neighbour_data = neighbour_data.reshape(9, face_width, 4, elem_count)
        current = face_update(
            current,
            volume,
            face_data,
            neighbour_data,
            orientation,
            normals,
            values,
            wave_speed,
            rotate,
            face_lift,
        )
    return current


def solution(mesh):
    return jax.shard_map(
        per_device,
        mesh=mesh,
        in_specs=(
            P(None, None, ("prow", "pcol")),
            P(),
            P(),
            P(),
            P(),
            P(),
            P(),
            P(("prow", "pcol")),
            P(None, None, ("prow", "pcol")),
            P(None, None, ("prow", "pcol")),
            P(None, ("prow", "pcol")),
            P(None, ("prow", "pcol")),
            P(None, ("prow", "pcol")),
            P("prow", "pcol", None, None),
            P("prow", "pcol", None, None),
        ),
        out_specs=P(None, None, ("prow", "pcol")),
        check_vma=False,
    )
```

```python
import jax
import jax.numpy as jnp
from jax import lax
from jax.sharding import PartitionSpec as P
from jax.experimental import pallas as pl

ORDER = 6
STEPS = 2


exact_mode = lax.Precision.HIGHEST
fast_mode = lax.Precision.HIGH
time_step = 0.8
OFFSETS = ((-1, -1), (-1, 0), (-1, 1), (0, -1), (0, 1), (1, -1), (1, 0), (1, 1))
ENTRIES = (
    (0, 0, 6, 0),
    (0, 1, 6, 1),
    (0, 2, 6, 1),
    (0, 3, 7, 2),
    (0, 5, 8, 2),
    (0, 6, 0, 3),
    (0, 7, 3, 3),
    (0, 8, 5, 3),
    (1, 0, 7, 1),
    (1, 1, 7, 0),
    (1, 2, 7, 1),
    (1, 3, 6, 2),
    (1, 4, 8, 2),
    (1, 6, 3, 3),
    (1, 7, 1, 3),
    (1, 8, 4, 3),
    (2, 0, 8, 1),
    (2, 1, 8, 1),
    (2, 2, 8, 0),
    (2, 4, 7, 2),
    (2, 5, 6, 2),
    (2, 6, 5, 3),
    (2, 7, 4, 3),
    (2, 8, 2, 3),
)


def shifted(x, axis, by):
    devices = lax.axis_size(axis)
    pairs = [(i, i + by) for i in range(devices) if 0 <= i + by < devices]
    return lax.ppermute(x, axis, pairs)


def element_params(material, material_id, normals):
    id_range = jnp.arange(material.shape[0], dtype=jnp.int32)
    chosen = material_id[None, None, :] == id_range[:, None, None]
    params = jnp.sum(jnp.where(chosen, material[:, :, None], 0.0), axis=0)
    density, lame_first, shear_modulus = (params[0], params[1], params[2])
    values = (-(lame_first + 2.0 * shear_modulus), -lame_first, -shear_modulus, -1.0 / density)
    wave_speed = jnp.sqrt((lame_first + 2.0 * shear_modulus) / density) * jnp.sum(
        jnp.abs(normals), axis=1
    )
    return (values, wave_speed)


def elastic_apply(parts, values):
    result = [None] * 9
    for comp_axis, row_index, col_index, kind_index in ENTRIES:
        term = values[kind_index] * parts[comp_axis][col_index]
        result[row_index] = term if result[row_index] is None else result[row_index] + term
    return jnp.stack(result, axis=0)


def star_apply(slopes, inv_jacobian, values):
    parts = [jnp.sum(inv_jacobian[:, k][:, None, None, :] * slopes, axis=0) for k in range(3)]
    return elastic_apply(parts, values)


def predict(current, inv_jacobian, values, grad_matrix):
    derivative = current
    integrated = time_step * current
    factor = time_step
    for power_level in range(1, ORDER):
        slopes = jnp.einsum("dab,qbe->dqae", grad_matrix, derivative, precision=fast_mode)
        derivative = -star_apply(slopes, inv_jacobian, values)
        factor = factor * time_step / (power_level + 1)
        integrated = integrated + factor * derivative
    return integrated


def predict_kernel(q_ref, jac_ref, val_ref, grad_ref, stiff_ref, integ_ref, qvol_ref):
    basis = q_ref.shape[1]
    lanes = q_ref.shape[2]
    jac = [[jac_ref[pl.ds(d * 3 + k, 1), :] for k in range(3)] for d in range(3)]
    vals = [val_ref[pl.ds(i, 1), :] for i in range(4)]
    coef = {}
    for d in range(3):
        for comp_axis, row_index, col_index, kind_index in ENTRIES:
            coef[(d, row_index, col_index)] = jac[d][comp_axis] * vals[kind_index]

    def apply(op, parts):
        stacked = jnp.concatenate(parts, axis=1)
        slopes = jnp.dot(op, stacked, precision=lax.Precision.HIGHEST, preferred_element_type=jnp.float32)
        out = [None] * 9
        for (d, row_index, col_index), c in coef.items():
            t = c * slopes[d * basis:(d + 1) * basis, col_index * lanes:(col_index + 1) * lanes]
            out[row_index] = t if out[row_index] is None else out[row_index] + t
        return out

    grad = grad_ref[...]
    derivative = [q_ref[q] for q in range(9)]
    integrated = [time_step * x for x in derivative]
    factor = time_step
    for level in range(1, ORDER):
        derivative = [-x for x in apply(grad, derivative)]
        factor = factor * time_step / (level + 1)
        integrated = [a + factor * b for a, b in zip(integrated, derivative)]
    for q in range(9):
        integ_ref[q] = integrated[q]
    volume = apply(stiff_ref[...], integrated)
    for q in range(9):
        qvol_ref[q] = q_ref[q] + volume[q]

def predict_call(current, jacobian_rows, value_rows, grad_rows, stiff_rows):
    shape = jax.ShapeDtypeStruct(current.shape, current.dtype)
    return pl.pallas_call(predict_kernel, out_shape=(shape, shape))(
        current, jacobian_rows, value_rows, grad_rows, stiff_rows
    )


def local_part(current, jacobian_rows, value_rows, grad_rows, stiff_rows, face_proj):
    integrated, advanced = predict_call(current, jacobian_rows, value_rows, grad_rows, stiff_rows)
    face_data = jnp.einsum("fib,qbe->qife", face_proj, integrated, precision=fast_mode)
    return (advanced, face_data)


def face_update(
    advanced,
    face_data,
    neighbour_data,
    orientation,
    normals,
    values,
    wave_speed,
    rotate,
    face_lift,
):
    turned = jnp.einsum("hil,qlfe->hqife", rotate, neighbour_data, precision=fast_mode)
    chosen = (orientation[None] == jnp.arange(3, dtype=jnp.int32)[:, None, None]).astype(
        advanced.dtype
    )
    turned = jnp.sum(turned * chosen[:, None, None, :, :], axis=0)
    both = face_data + turned
    apart = face_data - turned
    parts = [normals[:, k, :][None, None] * both for k in range(3)]
    flux_total = 0.5 * (elastic_apply(parts, values) + wave_speed[None, None] * apart)
    lifted = jnp.einsum("fai,pife->pae", face_lift, flux_total, precision=fast_mode)
    return advanced - lifted


SEND_ORDER = (0, 3, 5, 2, 4, 7, 1, 6)
RECV_ORDER = (4, 3, 6, 5, 7, 1, 0, 2)


def deliver(outgoing, slot_total):
    group = 3 * slot_total
    left = shifted(outgoing[:group], "pcol", -1)
    right = shifted(outgoing[group : 2 * group], "pcol", 1)
    up_bundle = jnp.concatenate(
        [outgoing[2 * group : 2 * group + slot_total], right[:slot_total], left[:slot_total]], axis=0
    )
    down_bundle = jnp.concatenate(
        [outgoing[2 * group + slot_total :], right[2 * slot_total :], left[2 * slot_total :]], axis=0
    )
    up = shifted(up_bundle, "prow", -1)
    down = shifted(down_bundle, "prow", 1)
    return jnp.concatenate(
        [left[slot_total : 2 * slot_total], right[slot_total : 2 * slot_total], up, down], axis=0
    )


def per_device(
    dof_values,
    grad_matrix,
    stiff_matrix,
    face_proj,
    face_lift,
    rotate,
    material,
    material_id,
    inv_jacobian,
    normals,
    orientation,
    neighbour,
    neighbour_face,
    send_list,
    recv_list,
):
    elem_count = dof_values.shape[2]
    face_width = face_proj.shape[1]
    face_total = 4 * elem_count
    dtype = dof_values.dtype
    values, wave_speed = element_params(material, material_id, normals)
    jacobian_rows = inv_jacobian.reshape(9, elem_count)
    value_rows = jnp.stack(values, axis=0)
    grad_rows = grad_matrix.reshape(-1, grad_matrix.shape[2])
    stiff_rows = stiff_matrix.reshape(-1, stiff_matrix.shape[2])
    face_ids = jnp.arange(face_total, dtype=jnp.int32)
    inside = (neighbour >= 0).reshape(-1)
    local_index = (neighbour_face * elem_count + jnp.maximum(neighbour, 0)).reshape(-1)
    gather_local = ((local_index[None, :] == face_ids[:, None]) & inside[None, :]).astype(dtype)
    source_ids = jnp.concatenate([send_list[0, 0, d : d + 1] for d in SEND_ORDER], axis=0)
    slot_total = source_ids.shape[1]
    gather_out = (source_ids.reshape(-1)[:, None] == face_ids[None, :]).astype(dtype)
    targets = jnp.concatenate([recv_list[0, 0, d] for d in RECV_ORDER], axis=0)
    scatter_in = ((targets[:, None] == face_ids[None, :]) & ~inside[None, :]).astype(dtype)
    current = dof_values
    for time_index in range(STEPS):
        advanced, face_data = local_part(
            current, jacobian_rows, value_rows, grad_rows, stiff_rows, face_proj
        )
        flat_faces = face_data.reshape(9 * face_width, face_total)
        outgoing = lax.dot_general(
            gather_out, flat_faces, (((1,), (1,)), ((), ())), precision=exact_mode
        )
        received = deliver(outgoing, slot_total)
        neighbour_data = jnp.dot(flat_faces, gather_local, precision=exact_mode) + lax.dot_general(
            received, scatter_in, (((0,), (0,)), ((), ())), precision=exact_mode
        )
        neighbour_data = neighbour_data.reshape(9, face_width, 4, elem_count)
        current = face_update(
            advanced,
            face_data,
            neighbour_data,
            orientation,
            normals,
            values,
            wave_speed,
            rotate,
            face_lift,
        )
    return current


def solution(mesh):
    return jax.shard_map(
        per_device,
        mesh=mesh,
        in_specs=(
            P(None, None, ("prow", "pcol")),
            P(),
            P(),
            P(),
            P(),
            P(),
            P(),
            P(("prow", "pcol")),
            P(None, None, ("prow", "pcol")),
            P(None, None, ("prow", "pcol")),
            P(None, ("prow", "pcol")),
            P(None, ("prow", "pcol")),
            P(None, ("prow", "pcol")),
            P("prow", "pcol", None, None),
            P("prow", "pcol", None, None),
        ),
        out_specs=P(None, None, ("prow", "pcol")),
        check_vma=False,
    )
```

```python
import jax
import jax.numpy as jnp
from jax import lax
from jax.sharding import PartitionSpec as P

ORDER = 6
STEPS = 2


exact_mode = lax.Precision.HIGHEST
fast_mode = lax.Precision.HIGH
time_step = 0.8
OFFSETS = ((-1, -1), (-1, 0), (-1, 1), (0, -1), (0, 1), (1, -1), (1, 0), (1, 1))
ENTRIES = (
    (0, 0, 6, 0),
    (0, 1, 6, 1),
    (0, 2, 6, 1),
    (0, 3, 7, 2),
    (0, 5, 8, 2),
    (0, 6, 0, 3),
    (0, 7, 3, 3),
    (0, 8, 5, 3),
    (1, 0, 7, 1),
    (1, 1, 7, 0),
    (1, 2, 7, 1),
    (1, 3, 6, 2),
    (1, 4, 8, 2),
    (1, 6, 3, 3),
    (1, 7, 1, 3),
    (1, 8, 4, 3),
    (2, 0, 8, 1),
    (2, 1, 8, 1),
    (2, 2, 8, 0),
    (2, 4, 7, 2),
    (2, 5, 6, 2),
    (2, 6, 5, 3),
    (2, 7, 4, 3),
    (2, 8, 2, 3),
)


def shifted(x, axis, by):
    devices = lax.axis_size(axis)
    pairs = [(i, i + by) for i in range(devices) if 0 <= i + by < devices]
    return lax.ppermute(x, axis, pairs)


def element_params(material, material_id, normals):
    id_range = jnp.arange(material.shape[0], dtype=jnp.int32)
    chosen = material_id[None, None, :] == id_range[:, None, None]
    params = jnp.sum(jnp.where(chosen, material[:, :, None], 0.0), axis=0)
    density, lame_first, shear_modulus = (params[0], params[1], params[2])
    values = (-(lame_first + 2.0 * shear_modulus), -lame_first, -shear_modulus, -1.0 / density)
    wave_speed = jnp.sqrt((lame_first + 2.0 * shear_modulus) / density) * jnp.sum(
        jnp.abs(normals), axis=1
    )
    return (values, wave_speed)


def elastic_apply(parts, values):
    result = [None] * 9
    for comp_axis, row_index, col_index, kind_index in ENTRIES:
        term = values[kind_index] * parts[comp_axis][col_index]
        result[row_index] = term if result[row_index] is None else result[row_index] + term
    return jnp.stack(result, axis=0)


def star_apply(slopes, inv_jacobian, values):
    parts = [jnp.sum(inv_jacobian[:, k][:, None, None, :] * slopes, axis=0) for k in range(3)]
    return elastic_apply(parts, values)


def predict(current, inv_jacobian, values, grad_matrix):
    derivative = current
    integrated = time_step * current
    factor = time_step
    for power_level in range(1, ORDER):
        slopes = jnp.einsum("dab,qbe->dqae", grad_matrix, derivative, precision=fast_mode)
        derivative = -star_apply(slopes, inv_jacobian, values)
        factor = factor * time_step / (power_level + 1)
        integrated = integrated + factor * derivative
    return integrated


def local_part(current, inv_jacobian, values, grad_matrix, stiff_matrix, face_proj):
    integrated = predict(current, inv_jacobian, values, grad_matrix)
    slopes = jnp.einsum("dab,qbe->dqae", stiff_matrix, integrated, precision=fast_mode)
    volume = star_apply(slopes, inv_jacobian, values)
    face_data = jnp.einsum("fib,qbe->qife", face_proj, integrated, precision=fast_mode)
    return (volume, face_data)


def rotated(neighbour_data, orientation, rotate):
    turned = jnp.einsum("hil,qlfe->hqife", rotate, neighbour_data, precision=fast_mode)
    chosen = (orientation[None] == jnp.arange(3, dtype=jnp.int32)[:, None, None]).astype(
        neighbour_data.dtype
    )
    return jnp.sum(turned * chosen[:, None, None, :, :], axis=0)


def lifted_flux(both, apart, normals, values, wave_speed, face_lift):
    parts = [normals[:, k, :][None, None] * both for k in range(3)]
    flux_total = 0.5 * (elastic_apply(parts, values) + wave_speed[None, None] * apart)
    return jnp.einsum("fai,pife->pae", face_lift, flux_total, precision=fast_mode)


SEND_ORDER = (0, 3, 5, 2, 4, 7, 1, 6)
RECV_ORDER = (4, 3, 6, 5, 7, 1, 0, 2)


def deliver(outgoing, slot_total):
    group = 3 * slot_total
    left = shifted(outgoing[:group], "pcol", -1)
    right = shifted(outgoing[group : 2 * group], "pcol", 1)
    up_bundle = jnp.concatenate(
        [outgoing[2 * group : 2 * group + slot_total], right[:slot_total], left[:slot_total]], axis=0
    )
    down_bundle = jnp.concatenate(
        [outgoing[2 * group + slot_total :], right[2 * slot_total :], left[2 * slot_total :]], axis=0
    )
    up = shifted(up_bundle, "prow", -1)
    down = shifted(down_bundle, "prow", 1)
    return jnp.concatenate(
        [left[slot_total : 2 * slot_total], right[slot_total : 2 * slot_total], up, down], axis=0
    )


def per_device(
    dof_values,
    grad_matrix,
    stiff_matrix,
    face_proj,
    face_lift,
    rotate,
    material,
    material_id,
    inv_jacobian,
    normals,
    orientation,
    neighbour,
    neighbour_face,
    send_list,
    recv_list,
):
    elem_count = dof_values.shape[2]
    face_width = face_proj.shape[1]
    face_total = 4 * elem_count
    dtype = dof_values.dtype
    values, wave_speed = element_params(material, material_id, normals)
    face_ids = jnp.arange(face_total, dtype=jnp.int32)
    inside = (neighbour >= 0).reshape(-1)
    local_index = (neighbour_face * elem_count + jnp.maximum(neighbour, 0)).reshape(-1)
    gather_local = ((local_index[None, :] == face_ids[:, None]) & inside[None, :]).astype(dtype)
    source_ids = jnp.concatenate([send_list[0, 0, d : d + 1] for d in SEND_ORDER], axis=0)
    slot_total = source_ids.shape[1]
    gather_out = (source_ids.reshape(-1)[:, None] == face_ids[None, :]).astype(dtype)
    targets = jnp.concatenate([recv_list[0, 0, d] for d in RECV_ORDER], axis=0)
    scatter_in = ((targets[:, None] == face_ids[None, :]) & ~inside[None, :]).astype(dtype)
    current = dof_values
    for time_index in range(STEPS):
        volume, face_data = local_part(
            current, inv_jacobian, values, grad_matrix, stiff_matrix, face_proj
        )
        flat_faces = face_data.reshape(9 * face_width, face_total)
        outgoing = lax.dot_general(
            gather_out, flat_faces, (((1,), (1,)), ((), ())), precision=exact_mode
        )
        local_turned = rotated(
            jnp.dot(flat_faces, gather_local, precision=exact_mode).reshape(
                9, face_width, 4, elem_count
            ),
            orientation,
            rotate,
        )
        advanced = current + volume - lifted_flux(
            face_data + local_turned,
            face_data - local_turned,
            normals,
            values,
            wave_speed,
            face_lift,
        )
        received = deliver(outgoing, slot_total)
        received, advanced = lax.optimization_barrier((received, advanced))
        remote_turned = rotated(
            lax.dot_general(
                received, scatter_in, (((0,), (0,)), ((), ())), precision=exact_mode
            ).reshape(9, face_width, 4, elem_count),
            orientation,
            rotate,
        )
        current = advanced - lifted_flux(
            remote_turned, -remote_turned, normals, values, wave_speed, face_lift
        )
    return current


def solution(mesh):
    return jax.shard_map(
        per_device,
        mesh=mesh,
        in_specs=(
            P(None, None, ("prow", "pcol")),
            P(),
            P(),
            P(),
            P(),
            P(),
            P(),
            P(("prow", "pcol")),
            P(None, None, ("prow", "pcol")),
            P(None, None, ("prow", "pcol")),
            P(None, ("prow", "pcol")),
            P(None, ("prow", "pcol")),
            P(None, ("prow", "pcol")),
            P("prow", "pcol", None, None),
            P("prow", "pcol", None, None),
        ),
        out_specs=P(None, None, ("prow", "pcol")),
        check_vma=False,
    )
```

```python
import jax
import jax.numpy as jnp
from jax import lax
from jax.sharding import PartitionSpec as P

ORDER = 6
STEPS = 2


exact_mode = lax.Precision.HIGHEST
fast_mode = lax.Precision.HIGH
time_step = 0.8
OFFSETS = ((-1, -1), (-1, 0), (-1, 1), (0, -1), (0, 1), (1, -1), (1, 0), (1, 1))
ENTRIES = (
    (0, 0, 6, 0),
    (0, 1, 6, 1),
    (0, 2, 6, 1),
    (0, 3, 7, 2),
    (0, 5, 8, 2),
    (0, 6, 0, 3),
    (0, 7, 3, 3),
    (0, 8, 5, 3),
    (1, 0, 7, 1),
    (1, 1, 7, 0),
    (1, 2, 7, 1),
    (1, 3, 6, 2),
    (1, 4, 8, 2),
    (1, 6, 3, 3),
    (1, 7, 1, 3),
    (1, 8, 4, 3),
    (2, 0, 8, 1),
    (2, 1, 8, 1),
    (2, 2, 8, 0),
    (2, 4, 7, 2),
    (2, 5, 6, 2),
    (2, 6, 5, 3),
    (2, 7, 4, 3),
    (2, 8, 2, 3),
)


def shifted(x, axis, by):
    devices = lax.axis_size(axis)
    pairs = [(i, i + by) for i in range(devices) if 0 <= i + by < devices]
    return lax.ppermute(x, axis, pairs)


def element_params(material, material_id, normals):
    id_range = jnp.arange(material.shape[0], dtype=jnp.int32)
    chosen = material_id[None, None, :] == id_range[:, None, None]
    params = jnp.sum(jnp.where(chosen, material[:, :, None], 0.0), axis=0)
    density, lame_first, shear_modulus = (params[0], params[1], params[2])
    values = (-(lame_first + 2.0 * shear_modulus), -lame_first, -shear_modulus, -1.0 / density)
    wave_speed = jnp.sqrt((lame_first + 2.0 * shear_modulus) / density) * jnp.sum(
        jnp.abs(normals), axis=1
    )
    return (values, wave_speed)


def elastic_apply(parts, values):
    result = [None] * 9
    for comp_axis, row_index, col_index, kind_index in ENTRIES:
        term = values[kind_index] * parts[comp_axis][col_index]
        result[row_index] = term if result[row_index] is None else result[row_index] + term
    return jnp.stack(result, axis=0)


def star_apply(slopes, inv_jacobian, values):
    parts = [jnp.sum(inv_jacobian[:, k][:, None, None, :] * slopes, axis=0) for k in range(3)]
    return elastic_apply(parts, values)


def predict(current, inv_jacobian, values, grad_matrix):
    derivative = current
    integrated = time_step * current
    factor = time_step
    for power_level in range(1, ORDER):
        slopes = jnp.einsum("dab,qbe->dqae", grad_matrix, derivative, precision=fast_mode)
        derivative = -star_apply(slopes, inv_jacobian, values)
        factor = factor * time_step / (power_level + 1)
        integrated = integrated + factor * derivative
    return integrated


def local_part(current, inv_jacobian, values, grad_matrix, stiff_matrix, face_proj):
    integrated = predict(current, inv_jacobian, values, grad_matrix)
    slopes = jnp.einsum("dab,qbe->dqae", stiff_matrix, integrated, precision=fast_mode)
    volume = star_apply(slopes, inv_jacobian, values)
    face_data = jnp.einsum("fib,qbe->qife", face_proj, integrated, precision=fast_mode)
    return (volume, face_data)


def face_update(
    current,
    volume,
    face_data,
    neighbour_data,
    orientation,
    normals,
    values,
    wave_speed,
    rotate,
    face_lift,
):
    turned = jnp.einsum("hil,qlfe->hqife", rotate, neighbour_data, precision=fast_mode)
    chosen = (orientation[None] == jnp.arange(3, dtype=jnp.int32)[:, None, None]).astype(
        current.dtype
    )
    turned = jnp.sum(turned * chosen[:, None, None, :, :], axis=0)
    both = face_data + turned
    apart = face_data - turned
    parts = [normals[:, k, :][None, None] * both for k in range(3)]
    flux_total = 0.5 * (elastic_apply(parts, values) + wave_speed[None, None] * apart)
    lifted = jnp.einsum("fai,pife->pae", face_lift, flux_total, precision=fast_mode)
    return current + volume - lifted


SEND_ORDER = (0, 3, 5, 2, 4, 7, 1, 6)


def deliver(outgoing, slot_total):
    group = 3 * slot_total
    left = shifted(outgoing[:group], "pcol", -1)
    right = shifted(outgoing[group : 2 * group], "pcol", 1)
    up_bundle = jnp.concatenate(
        [right[:slot_total], outgoing[2 * group : 2 * group + slot_total], left[:slot_total]], axis=0
    )
    down_bundle = jnp.concatenate(
        [right[2 * slot_total :], outgoing[2 * group + slot_total :], left[2 * slot_total :]], axis=0
    )
    up = shifted(up_bundle, "prow", -1)
    down = shifted(down_bundle, "prow", 1)
    return jnp.concatenate(
        [down, right[slot_total : 2 * slot_total], left[slot_total : 2 * slot_total], up], axis=0
    )


def per_device(
    dof_values,
    grad_matrix,
    stiff_matrix,
    face_proj,
    face_lift,
    rotate,
    material,
    material_id,
    inv_jacobian,
    normals,
    orientation,
    neighbour,
    neighbour_face,
    send_list,
    recv_list,
):
    elem_count = dof_values.shape[2]
    face_width = face_proj.shape[1]
    face_total = 4 * elem_count
    dtype = dof_values.dtype
    values, wave_speed = element_params(material, material_id, normals)
    face_ids = jnp.arange(face_total, dtype=jnp.int32)
    inside = (neighbour >= 0).reshape(-1)
    local_index = (neighbour_face * elem_count + jnp.maximum(neighbour, 0)).reshape(-1)
    gather_local = ((local_index[None, :] == face_ids[:, None]) & inside[None, :]).astype(dtype)
    source_ids = jnp.concatenate([send_list[0, 0, d : d + 1] for d in SEND_ORDER], axis=0)
    slot_total = source_ids.shape[1]
    gather_out = (source_ids.reshape(-1)[:, None] == face_ids[None, :]).astype(dtype)
    targets = recv_list[0, 0].reshape(-1)
    scatter_in = ((targets[:, None] == face_ids[None, :]) & ~inside[None, :]).astype(dtype)
    current = dof_values
    for time_index in range(STEPS):
        volume, face_data = local_part(
            current, inv_jacobian, values, grad_matrix, stiff_matrix, face_proj
        )
        flat_faces = face_data.reshape(9 * face_width, face_total)
        outgoing = lax.dot_general(
            gather_out, flat_faces, (((1,), (1,)), ((), ())), precision=exact_mode
        )
        received = deliver(outgoing, slot_total)
        neighbour_data = jnp.dot(flat_faces, gather_local, precision=exact_mode) + lax.dot_general(
            received, scatter_in, (((0,), (0,)), ((), ())), precision=exact_mode
        )
        neighbour_data = neighbour_data.reshape(9, face_width, 4, elem_count)
        current = face_update(
            current,
            volume,
            face_data,
            neighbour_data,
            orientation,
            normals,
            values,
            wave_speed,
            rotate,
            face_lift,
        )
    return current


def solution(mesh):
    return jax.shard_map(
        per_device,
        mesh=mesh,
        in_specs=(
            P(None, None, ("prow", "pcol")),
            P(),
            P(),
            P(),
            P(),
            P(),
            P(),
            P(("prow", "pcol")),
            P(None, None, ("prow", "pcol")),
            P(None, None, ("prow", "pcol")),
            P(None, ("prow", "pcol")),
            P(None, ("prow", "pcol")),
            P(None, ("prow", "pcol")),
            P("prow", "pcol", None, None),
            P("prow", "pcol", None, None),
        ),
        out_specs=P(None, None, ("prow", "pcol")),
        check_vma=False,
    )
```

```python
import jax
import jax.numpy as jnp
from jax import lax
from jax.sharding import PartitionSpec as P

ORDER = 6
STEPS = 2


exact_mode = lax.Precision.HIGHEST
fast_mode = lax.Precision.HIGH
time_step = 0.8
OFFSETS = ((-1, -1), (-1, 0), (-1, 1), (0, -1), (0, 1), (1, -1), (1, 0), (1, 1))
ENTRIES = (
    (0, 0, 6, 0),
    (0, 1, 6, 1),
    (0, 2, 6, 1),
    (0, 3, 7, 2),
    (0, 5, 8, 2),
    (0, 6, 0, 3),
    (0, 7, 3, 3),
    (0, 8, 5, 3),
    (1, 0, 7, 1),
    (1, 1, 7, 0),
    (1, 2, 7, 1),
    (1, 3, 6, 2),
    (1, 4, 8, 2),
    (1, 6, 3, 3),
    (1, 7, 1, 3),
    (1, 8, 4, 3),
    (2, 0, 8, 1),
    (2, 1, 8, 1),
    (2, 2, 8, 0),
    (2, 4, 7, 2),
    (2, 5, 6, 2),
    (2, 6, 5, 3),
    (2, 7, 4, 3),
    (2, 8, 2, 3),
)


def shifted(x, axis, by):
    devices = lax.axis_size(axis)
    pairs = [(i, i + by) for i in range(devices) if 0 <= i + by < devices]
    return lax.ppermute(x, axis, pairs)


def element_params(material, material_id, normals):
    id_range = jnp.arange(material.shape[0], dtype=jnp.int32)
    chosen = material_id[None, None, :] == id_range[:, None, None]
    params = jnp.sum(jnp.where(chosen, material[:, :, None], 0.0), axis=0)
    density, lame_first, shear_modulus = (params[0], params[1], params[2])
    values = (-(lame_first + 2.0 * shear_modulus), -lame_first, -shear_modulus, -1.0 / density)
    wave_speed = jnp.sqrt((lame_first + 2.0 * shear_modulus) / density) * jnp.sum(
        jnp.abs(normals), axis=1
    )
    return (values, wave_speed)


def elastic_apply(parts, values):
    result = [None] * 9
    for comp_axis, row_index, col_index, kind_index in ENTRIES:
        term = values[kind_index] * parts[comp_axis][col_index]
        result[row_index] = term if result[row_index] is None else result[row_index] + term
    return jnp.stack(result, axis=0)


def star_apply(slopes, inv_jacobian, values):
    parts = [jnp.sum(inv_jacobian[:, k][:, None, None, :] * slopes, axis=0) for k in range(3)]
    return elastic_apply(parts, values)


def predict(current, inv_jacobian, values, grad_matrix):
    derivative = current
    integrated = time_step * current
    factor = time_step
    for power_level in range(1, ORDER):
        slopes = jnp.einsum("dab,qbe->dqae", grad_matrix, derivative, precision=fast_mode)
        derivative = -star_apply(slopes, inv_jacobian, values)
        factor = factor * time_step / (power_level + 1)
        integrated = integrated + factor * derivative
    return integrated


def local_part(current, inv_jacobian, values, grad_matrix, stiff_matrix, face_proj):
    integrated = predict(current, inv_jacobian, values, grad_matrix)
    slopes = jnp.einsum("dab,qbe->dqae", stiff_matrix, integrated, precision=fast_mode)
    volume = star_apply(slopes, inv_jacobian, values)
    face_data = jnp.einsum("fib,qbe->qife", face_proj, integrated, precision=fast_mode)
    return (volume, face_data)


def face_update(
    current,
    volume,
    face_data,
    neighbour_data,
    orientation,
    normals,
    values,
    wave_speed,
    rotate,
    face_lift,
):
    turned = jnp.einsum("hil,qlfe->hqife", rotate, neighbour_data, precision=fast_mode)
    chosen = (orientation[None] == jnp.arange(3, dtype=jnp.int32)[:, None, None]).astype(
        current.dtype
    )
    turned = jnp.sum(turned * chosen[:, None, None, :, :], axis=0)
    both = face_data + turned
    apart = face_data - turned
    parts = [normals[:, k, :][None, None] * both for k in range(3)]
    flux_total = 0.5 * (elastic_apply(parts, values) + wave_speed[None, None] * apart)
    lifted = jnp.einsum("fai,pife->pae", face_lift, flux_total, precision=fast_mode)
    return current + volume - lifted


SEND_ORDER = (0, 1, 2, 5, 6, 7, 3, 4)
RECV_ORDER = (4, 7, 2, 3, 5, 0, 6, 1)


def deliver(outgoing, slot_total):
    group = 3 * slot_total
    up = shifted(outgoing[:group], "prow", -1)
    down = shifted(outgoing[group : 2 * group], "prow", 1)
    left_bundle = jnp.concatenate(
        [outgoing[2 * group : 2 * group + slot_total], up[:slot_total], down[:slot_total]], axis=0
    )
    right_bundle = jnp.concatenate(
        [outgoing[2 * group + slot_total :], up[2 * slot_total :], down[2 * slot_total :]], axis=0
    )
    left = shifted(left_bundle, "pcol", -1)
    right = shifted(right_bundle, "pcol", 1)
    return jnp.concatenate(
        [left, right, up[slot_total : 2 * slot_total], down[slot_total : 2 * slot_total]], axis=0
    )


def per_device(
    dof_values,
    grad_matrix,
    stiff_matrix,
    face_proj,
    face_lift,
    rotate,
    material,
    material_id,
    inv_jacobian,
    normals,
    orientation,
    neighbour,
    neighbour_face,
    send_list,
    recv_list,
):
    elem_count = dof_values.shape[2]
    face_width = face_proj.shape[1]
    face_total = 4 * elem_count
    dtype = dof_values.dtype
    values, wave_speed = element_params(material, material_id, normals)
    face_ids = jnp.arange(face_total, dtype=jnp.int32)
    inside = (neighbour >= 0).reshape(-1)
    local_index = (neighbour_face * elem_count + jnp.maximum(neighbour, 0)).reshape(-1)
    gather_local = ((local_index[None, :] == face_ids[:, None]) & inside[None, :]).astype(dtype)
    source_ids = jnp.concatenate([send_list[0, 0, d : d + 1] for d in SEND_ORDER], axis=0)
    slot_total = source_ids.shape[1]
    gather_out = (source_ids.reshape(-1)[:, None] == face_ids[None, :]).astype(dtype)
    targets = jnp.concatenate([recv_list[0, 0, d] for d in RECV_ORDER], axis=0)
    scatter_in = ((targets[:, None] == face_ids[None, :]) & ~inside[None, :]).astype(dtype)
    current = dof_values
    for time_index in range(STEPS):
        volume, face_data = local_part(
            current, inv_jacobian, values, grad_matrix, stiff_matrix, face_proj
        )
        flat_faces = face_data.reshape(9 * face_width, face_total)
        outgoing = lax.dot_general(
            gather_out, flat_faces, (((1,), (1,)), ((), ())), precision=exact_mode
        )
        received = deliver(outgoing, slot_total)
        neighbour_data = jnp.dot(flat_faces, gather_local, precision=exact_mode) + lax.dot_general(
            received, scatter_in, (((0,), (0,)), ((), ())), precision=exact_mode
        )
        neighbour_data = neighbour_data.reshape(9, face_width, 4, elem_count)
        current = face_update(
            current,
            volume,
            face_data,
            neighbour_data,
            orientation,
            normals,
            values,
            wave_speed,
            rotate,
            face_lift,
        )
    return current


def solution(mesh):
    return jax.shard_map(
        per_device,
        mesh=mesh,
        in_specs=(
            P(None, None, ("prow", "pcol")),
            P(),
            P(),
            P(),
            P(),
            P(),
            P(),
            P(("prow", "pcol")),
            P(None, None, ("prow", "pcol")),
            P(None, None, ("prow", "pcol")),
            P(None, ("prow", "pcol")),
            P(None, ("prow", "pcol")),
            P(None, ("prow", "pcol")),
            P("prow", "pcol", None, None),
            P("prow", "pcol", None, None),
        ),
        out_specs=P(None, None, ("prow", "pcol")),
        check_vma=False,
    )
```

```python
import jax
import jax.numpy as jnp
from jax import lax
from jax.sharding import PartitionSpec as P

ORDER = 6
STEPS = 2


exact_mode = lax.Precision.HIGHEST
fast_mode = lax.Precision.HIGH
time_step = 0.8
OFFSETS = ((-1, -1), (-1, 0), (-1, 1), (0, -1), (0, 1), (1, -1), (1, 0), (1, 1))
ENTRIES = (
    (0, 0, 6, 0),
    (0, 1, 6, 1),
    (0, 2, 6, 1),
    (0, 3, 7, 2),
    (0, 5, 8, 2),
    (0, 6, 0, 3),
    (0, 7, 3, 3),
    (0, 8, 5, 3),
    (1, 0, 7, 1),
    (1, 1, 7, 0),
    (1, 2, 7, 1),
    (1, 3, 6, 2),
    (1, 4, 8, 2),
    (1, 6, 3, 3),
    (1, 7, 1, 3),
    (1, 8, 4, 3),
    (2, 0, 8, 1),
    (2, 1, 8, 1),
    (2, 2, 8, 0),
    (2, 4, 7, 2),
    (2, 5, 6, 2),
    (2, 6, 5, 3),
    (2, 7, 4, 3),
    (2, 8, 2, 3),
)


def shifted(x, axis, by):
    devices = lax.axis_size(axis)
    pairs = [(i, i + by) for i in range(devices) if 0 <= i + by < devices]
    return lax.ppermute(x, axis, pairs)


def element_params(material, material_id, normals):
    id_range = jnp.arange(material.shape[0], dtype=jnp.int32)
    chosen = material_id[None, None, :] == id_range[:, None, None]
    params = jnp.sum(jnp.where(chosen, material[:, :, None], 0.0), axis=0)
    density, lame_first, shear_modulus = (params[0], params[1], params[2])
    values = (-(lame_first + 2.0 * shear_modulus), -lame_first, -shear_modulus, -1.0 / density)
    wave_speed = jnp.sqrt((lame_first + 2.0 * shear_modulus) / density) * jnp.sum(
        jnp.abs(normals), axis=1
    )
    return (values, wave_speed)


def elastic_apply(parts, values):
    result = [None] * 9
    for comp_axis, row_index, col_index, kind_index in ENTRIES:
        term = values[kind_index] * parts[comp_axis][col_index]
        result[row_index] = term if result[row_index] is None else result[row_index] + term
    return jnp.stack(result, axis=0)


def star_apply(slopes, inv_jacobian, values):
    parts = [jnp.sum(inv_jacobian[:, k][:, None, None, :] * slopes, axis=0) for k in range(3)]
    return elastic_apply(parts, values)


def predict(current, inv_jacobian, values, grad_matrix):
    derivative = current
    integrated = time_step * current
    factor = time_step
    for power_level in range(1, ORDER):
        slopes = jnp.einsum("dab,qbe->dqae", grad_matrix, derivative, precision=fast_mode)
        derivative = -star_apply(slopes, inv_jacobian, values)
        factor = factor * time_step / (power_level + 1)
        integrated = integrated + factor * derivative
    return integrated


def local_part(current, inv_jacobian, values, grad_matrix, face_proj):
    integrated = predict(current, inv_jacobian, values, grad_matrix)
    face_data = jnp.einsum("fib,qbe->qife", face_proj, integrated, precision=fast_mode)
    return (integrated, face_data)


def face_update(
    current,
    volume,
    face_data,
    neighbour_data,
    orientation,
    normals,
    values,
    wave_speed,
    rotate,
    face_lift,
):
    turned = jnp.einsum("hil,qlfe->hqife", rotate, neighbour_data, precision=fast_mode)
    chosen = (orientation[None] == jnp.arange(3, dtype=jnp.int32)[:, None, None]).astype(
        current.dtype
    )
    turned = jnp.sum(turned * chosen[:, None, None, :, :], axis=0)
    both = face_data + turned
    apart = face_data - turned
    parts = [normals[:, k, :][None, None] * both for k in range(3)]
    flux_total = 0.5 * (elastic_apply(parts, values) + wave_speed[None, None] * apart)
    lifted = jnp.einsum("fai,pife->pae", face_lift, flux_total, precision=fast_mode)
    return current + volume - lifted


SEND_ORDER = (0, 3, 5, 2, 4, 7, 1, 6)


def deliver(outgoing, slot_total, deferred, local_work):
    group = 3 * slot_total
    left = shifted(outgoing[:group], "pcol", -1)
    right = shifted(outgoing[group : 2 * group], "pcol", 1)
    left, right, deferred = lax.optimization_barrier((left, right, deferred))
    finished = local_work(*deferred)
    up_bundle = jnp.concatenate(
        [right[:slot_total], outgoing[2 * group : 2 * group + slot_total], left[:slot_total]], axis=0
    )
    down_bundle = jnp.concatenate(
        [right[2 * slot_total :], outgoing[2 * group + slot_total :], left[2 * slot_total :]], axis=0
    )
    up = shifted(up_bundle, "prow", -1)
    down = shifted(down_bundle, "prow", 1)
    up, down, finished = lax.optimization_barrier((up, down, finished))
    return jnp.concatenate(
        [down, right[slot_total : 2 * slot_total], left[slot_total : 2 * slot_total], up], axis=0
    ), finished


def per_device(
    dof_values,
    grad_matrix,
    stiff_matrix,
    face_proj,
    face_lift,
    rotate,
    material,
    material_id,
    inv_jacobian,
    normals,
    orientation,
    neighbour,
    neighbour_face,
    send_list,
    recv_list,
):
    elem_count = dof_values.shape[2]
    face_width = face_proj.shape[1]
    face_total = 4 * elem_count
    dtype = dof_values.dtype
    values, wave_speed = element_params(material, material_id, normals)
    face_ids = jnp.arange(face_total, dtype=jnp.int32)
    inside = (neighbour >= 0).reshape(-1)
    local_index = (neighbour_face * elem_count + jnp.maximum(neighbour, 0)).reshape(-1)
    gather_local = ((local_index[None, :] == face_ids[:, None]) & inside[None, :]).astype(dtype)
    source_ids = jnp.concatenate([send_list[0, 0, d : d + 1] for d in SEND_ORDER], axis=0)
    slot_total = source_ids.shape[1]
    gather_out = (source_ids.reshape(-1)[:, None] == face_ids[None, :]).astype(dtype)
    targets = recv_list[0, 0].reshape(-1)
    scatter_in = ((targets[:, None] == face_ids[None, :]) & ~inside[None, :]).astype(dtype)
    current = dof_values
    for time_index in range(STEPS):
        integrated, face_data = local_part(
            current, inv_jacobian, values, grad_matrix, face_proj
        )
        flat_faces = face_data.reshape(9 * face_width, face_total)
        outgoing = lax.dot_general(
            gather_out, flat_faces, (((1,), (1,)), ((), ())), precision=exact_mode
        )

        def local_work(integrated, flat_faces):
            slopes = jnp.einsum("dab,qbe->dqae", stiff_matrix, integrated, precision=fast_mode)
            volume = star_apply(slopes, inv_jacobian, values)
            local_data = jnp.dot(flat_faces, gather_local, precision=exact_mode)
            return volume, local_data

        received, (volume, local_data) = deliver(
            outgoing, slot_total, (integrated, flat_faces), local_work
        )
        neighbour_data = local_data + lax.dot_general(
            received, scatter_in, (((0,), (0,)), ((), ())), precision=exact_mode
        )
        neighbour_data = neighbour_data.reshape(9, face_width, 4, elem_count)
        current = face_update(
            current,
            volume,
            face_data,
            neighbour_data,
            orientation,
            normals,
            values,
            wave_speed,
            rotate,
            face_lift,
        )
    return current


def solution(mesh):
    return jax.shard_map(
        per_device,
        mesh=mesh,
        in_specs=(
            P(None, None, ("prow", "pcol")),
            P(),
            P(),
            P(),
            P(),
            P(),
            P(),
            P(("prow", "pcol")),
            P(None, None, ("prow", "pcol")),
            P(None, None, ("prow", "pcol")),
            P(None, ("prow", "pcol")),
            P(None, ("prow", "pcol")),
            P(None, ("prow", "pcol")),
            P("prow", "pcol", None, None),
            P("prow", "pcol", None, None),
        ),
        out_specs=P(None, None, ("prow", "pcol")),
        check_vma=False,
    )
```

```python
import jax
import jax.numpy as jnp
from jax import lax
from jax.sharding import PartitionSpec as P

ORDER = 6
STEPS = 2


exact_mode = lax.Precision.HIGHEST
fast_mode = lax.Precision.HIGH
time_step = 0.8
OFFSETS = ((-1, -1), (-1, 0), (-1, 1), (0, -1), (0, 1), (1, -1), (1, 0), (1, 1))
ENTRIES = (
    (0, 0, 6, 0),
    (0, 1, 6, 1),
    (0, 2, 6, 1),
    (0, 3, 7, 2),
    (0, 5, 8, 2),
    (0, 6, 0, 3),
    (0, 7, 3, 3),
    (0, 8, 5, 3),
    (1, 0, 7, 1),
    (1, 1, 7, 0),
    (1, 2, 7, 1),
    (1, 3, 6, 2),
    (1, 4, 8, 2),
    (1, 6, 3, 3),
    (1, 7, 1, 3),
    (1, 8, 4, 3),
    (2, 0, 8, 1),
    (2, 1, 8, 1),
    (2, 2, 8, 0),
    (2, 4, 7, 2),
    (2, 5, 6, 2),
    (2, 6, 5, 3),
    (2, 7, 4, 3),
    (2, 8, 2, 3),
)


def shifted(x, axis, by):
    devices = lax.axis_size(axis)
    pairs = [(i, i + by) for i in range(devices) if 0 <= i + by < devices]
    return lax.ppermute(x, axis, pairs)


def element_params(material, material_id, normals):
    id_range = jnp.arange(material.shape[0], dtype=jnp.int32)
    chosen = material_id[None, None, :] == id_range[:, None, None]
    params = jnp.sum(jnp.where(chosen, material[:, :, None], 0.0), axis=0)
    density, lame_first, shear_modulus = (params[0], params[1], params[2])
    values = (-(lame_first + 2.0 * shear_modulus), -lame_first, -shear_modulus, -1.0 / density)
    wave_speed = jnp.sqrt((lame_first + 2.0 * shear_modulus) / density) * jnp.sum(
        jnp.abs(normals), axis=1
    )
    return (values, wave_speed)


def elastic_apply(parts, values):
    result = [None] * 9
    for comp_axis, row_index, col_index, kind_index in ENTRIES:
        term = values[kind_index] * parts[comp_axis][col_index]
        result[row_index] = term if result[row_index] is None else result[row_index] + term
    return jnp.stack(result, axis=0)


def star_apply(slopes, inv_jacobian, values):
    parts = [jnp.sum(inv_jacobian[:, k][:, None, None, :] * slopes, axis=0) for k in range(3)]
    return elastic_apply(parts, values)


def predict(current, inv_jacobian, values, grad_matrix):
    derivative = current
    integrated = time_step * current
    factor = time_step
    for power_level in range(1, ORDER):
        slopes = jnp.einsum("dab,qbe->dqae", grad_matrix, derivative, precision=fast_mode)
        derivative = -star_apply(slopes, inv_jacobian, values)
        factor = factor * time_step / (power_level + 1)
        integrated = integrated + factor * derivative
    return integrated


def local_part(current, inv_jacobian, values, grad_matrix, face_proj):
    integrated = predict(current, inv_jacobian, values, grad_matrix)
    face_data = jnp.einsum("fib,qbe->qife", face_proj, integrated, precision=fast_mode)
    return (integrated, face_data)


def face_update(
    current,
    volume,
    face_data,
    neighbour_data,
    orientation,
    normals,
    values,
    wave_speed,
    rotate_negated,
    half_lift,
):
    turned_negated = jnp.einsum(
        "hil,qlfe->hqife", rotate_negated, neighbour_data, precision=fast_mode
    )
    chosen = (orientation[None] == jnp.arange(3, dtype=jnp.int32)[:, None, None]).astype(
        current.dtype
    )
    turned_negated = jnp.sum(turned_negated * chosen[:, None, None, :, :], axis=0)
    both = face_data - turned_negated
    apart = face_data + turned_negated
    parts = [normals[:, k, :][None, None] * both for k in range(3)]
    flux_total = elastic_apply(parts, values) + wave_speed[None, None] * apart
    lifted = jnp.einsum("fai,pife->pae", half_lift, flux_total, precision=fast_mode)
    return current + volume - lifted


SEND_ORDER = (0, 3, 5, 2, 4, 7, 1, 6)


def deliver(outgoing, slot_total, deferred, local_work):
    group = 3 * slot_total
    left = shifted(outgoing[:group], "pcol", -1)
    right = shifted(outgoing[group : 2 * group], "pcol", 1)
    left, right, deferred = lax.optimization_barrier((left, right, deferred))
    finished = local_work(*deferred)
    up_bundle = jnp.concatenate(
        [right[:slot_total], outgoing[2 * group : 2 * group + slot_total], left[:slot_total]], axis=0
    )
    down_bundle = jnp.concatenate(
        [right[2 * slot_total :], outgoing[2 * group + slot_total :], left[2 * slot_total :]], axis=0
    )
    up = shifted(up_bundle, "prow", -1)
    down = shifted(down_bundle, "prow", 1)
    up, down, finished = lax.optimization_barrier((up, down, finished))
    return jnp.concatenate(
        [down, right[slot_total : 2 * slot_total], left[slot_total : 2 * slot_total], up], axis=0
    ), finished


def per_device(
    dof_values,
    grad_matrix,
    stiff_matrix,
    face_proj,
    face_lift,
    rotate,
    material,
    material_id,
    inv_jacobian,
    normals,
    orientation,
    neighbour,
    neighbour_face,
    send_list,
    recv_list,
):
    elem_count = dof_values.shape[2]
    face_width = face_proj.shape[1]
    face_total = 4 * elem_count
    dtype = dof_values.dtype
    values, wave_speed = element_params(material, material_id, normals)
    face_ids = jnp.arange(face_total, dtype=jnp.int32)
    inside = (neighbour >= 0).reshape(-1)
    local_index = (neighbour_face * elem_count + jnp.maximum(neighbour, 0)).reshape(-1)
    gather_local = ((local_index[None, :] == face_ids[:, None]) & inside[None, :]).astype(dtype)
    source_ids = jnp.concatenate([send_list[0, 0, d : d + 1] for d in SEND_ORDER], axis=0)
    slot_total = source_ids.shape[1]
    gather_out = (source_ids.reshape(-1)[:, None] == face_ids[None, :]).astype(dtype)
    targets = recv_list[0, 0].reshape(-1)
    scatter_in = ((targets[:, None] == face_ids[None, :]) & ~inside[None, :]).astype(dtype)
    current = dof_values
    rotate_negated, half_lift = rotate, face_lift
    for time_index in range(STEPS):
        integrated, face_data = local_part(
            current, inv_jacobian, values, grad_matrix, face_proj
        )
        flat_faces = face_data.reshape(9 * face_width, face_total)
        outgoing = lax.dot_general(
            gather_out, flat_faces, (((1,), (1,)), ((), ())), precision=exact_mode
        )

        def local_work(integrated, flat_faces, rotate_negated, half_lift):
            slopes = jnp.einsum("dab,qbe->dqae", stiff_matrix, integrated, precision=fast_mode)
            volume = star_apply(slopes, inv_jacobian, values)
            local_data = jnp.dot(flat_faces, gather_local, precision=exact_mode)
            if time_index == 0:
                rotate_negated = -rotate_negated
                half_lift = 0.5 * half_lift
            return volume, local_data, rotate_negated, half_lift

        received, (volume, local_data, rotate_negated, half_lift) = deliver(
            outgoing, slot_total, (integrated, flat_faces, rotate_negated, half_lift), local_work
        )
        neighbour_data = local_data + lax.dot_general(
            received, scatter_in, (((0,), (0,)), ((), ())), precision=exact_mode
        )
        neighbour_data = neighbour_data.reshape(9, face_width, 4, elem_count)
        current = face_update(
            current,
            volume,
            face_data,
            neighbour_data,
            orientation,
            normals,
            values,
            wave_speed,
            rotate_negated,
            half_lift,
        )
    return current


def solution(mesh):
    return jax.shard_map(
        per_device,
        mesh=mesh,
        in_specs=(
            P(None, None, ("prow", "pcol")),
            P(),
            P(),
            P(),
            P(),
            P(),
            P(),
            P(("prow", "pcol")),
            P(None, None, ("prow", "pcol")),
            P(None, None, ("prow", "pcol")),
            P(None, ("prow", "pcol")),
            P(None, ("prow", "pcol")),
            P(None, ("prow", "pcol")),
            P("prow", "pcol", None, None),
            P("prow", "pcol", None, None),
        ),
        out_specs=P(None, None, ("prow", "pcol")),
        check_vma=False,
    )
```

```python
import jax
import jax.numpy as jnp
from jax import lax
from jax.sharding import PartitionSpec as P

ORDER = 6
STEPS = 2


exact_mode = lax.Precision.HIGHEST
fast_mode = lax.Precision.HIGH
time_step = 0.8
OFFSETS = ((-1, -1), (-1, 0), (-1, 1), (0, -1), (0, 1), (1, -1), (1, 0), (1, 1))
ENTRIES = (
    (0, 0, 6, 0),
    (0, 1, 6, 1),
    (0, 2, 6, 1),
    (0, 3, 7, 2),
    (0, 5, 8, 2),
    (0, 6, 0, 3),
    (0, 7, 3, 3),
    (0, 8, 5, 3),
    (1, 0, 7, 1),
    (1, 1, 7, 0),
    (1, 2, 7, 1),
    (1, 3, 6, 2),
    (1, 4, 8, 2),
    (1, 6, 3, 3),
    (1, 7, 1, 3),
    (1, 8, 4, 3),
    (2, 0, 8, 1),
    (2, 1, 8, 1),
    (2, 2, 8, 0),
    (2, 4, 7, 2),
    (2, 5, 6, 2),
    (2, 6, 5, 3),
    (2, 7, 4, 3),
    (2, 8, 2, 3),
)


def shifted(x, axis, by):
    devices = lax.axis_size(axis)
    pairs = [(i, i + by) for i in range(devices) if 0 <= i + by < devices]
    return lax.ppermute(x, axis, pairs)


def element_params(material, material_id, normals):
    id_range = jnp.arange(material.shape[0], dtype=jnp.int32)
    chosen = material_id[None, None, :] == id_range[:, None, None]
    params = jnp.sum(jnp.where(chosen, material[:, :, None], 0.0), axis=0)
    density, lame_first, shear_modulus = (params[0], params[1], params[2])
    values = (-(lame_first + 2.0 * shear_modulus), -lame_first, -shear_modulus, -1.0 / density)
    wave_speed = jnp.sqrt((lame_first + 2.0 * shear_modulus) / density) * jnp.sum(
        jnp.abs(normals), axis=1
    )
    return (values, wave_speed)


def elastic_apply(parts, values):
    result = [None] * 9
    for comp_axis, row_index, col_index, kind_index in ENTRIES:
        term = values[kind_index] * parts[comp_axis][col_index]
        result[row_index] = term if result[row_index] is None else result[row_index] + term
    return jnp.stack(result, axis=0)


def star_apply(slopes, inv_jacobian, values):
    parts = [jnp.sum(inv_jacobian[:, k][:, None, None, :] * slopes, axis=0) for k in range(3)]
    return elastic_apply(parts, values)


def predict(current, inv_jacobian, values, grad_matrix):
    derivative = current
    integrated = time_step * current
    factor = time_step
    for power_level in range(1, ORDER):
        slopes = jnp.einsum("dab,qbe->dqae", grad_matrix, derivative, precision=fast_mode)
        derivative = -star_apply(slopes, inv_jacobian, values)
        factor = factor * time_step / (power_level + 1)
        integrated = integrated + factor * derivative
    return integrated


def local_part(current, inv_jacobian, values, grad_matrix, face_proj):
    integrated = predict(current, inv_jacobian, values, grad_matrix)
    face_data = jnp.einsum("fib,qbe->qife", face_proj, integrated, precision=fast_mode)
    return (integrated, face_data)


def rotate_faces(neighbour_data, orientation, rotate_negated):
    turned_negated = jnp.einsum(
        "hil,qlfe->hqife", rotate_negated, neighbour_data, precision=fast_mode
    )
    chosen = (orientation[None] == jnp.arange(3, dtype=jnp.int32)[:, None, None]).astype(
        neighbour_data.dtype
    )
    return jnp.sum(turned_negated * chosen[:, None, None, :, :], axis=0)


def rotate_slots(received, slot_chosen, rotate_negated, face_width):
    slots = received.reshape(received.shape[0], -1, face_width)
    turned_negated = jnp.einsum("hil,sql->hsqi", rotate_negated, slots, precision=fast_mode)
    turned_negated = jnp.sum(turned_negated * slot_chosen[:, :, None, None], axis=0)
    return turned_negated.reshape(received.shape)


def face_update(
    current,
    volume,
    face_data,
    turned_negated,
    normals,
    values,
    wave_speed,
    half_lift,
):
    both = face_data - turned_negated
    apart = face_data + turned_negated
    parts = [normals[:, k, :][None, None] * both for k in range(3)]
    flux_total = elastic_apply(parts, values) + wave_speed[None, None] * apart
    lifted = jnp.einsum("fai,pife->pae", half_lift, flux_total, precision=fast_mode)
    return current + volume - lifted


SEND_ORDER = (0, 3, 5, 2, 4, 7, 1, 6)


def deliver(outgoing, slot_total, deferred, local_work):
    group = 3 * slot_total
    left = shifted(outgoing[:group], "pcol", -1)
    right = shifted(outgoing[group : 2 * group], "pcol", 1)
    left, right, deferred = lax.optimization_barrier((left, right, deferred))
    finished = local_work(*deferred)
    up_bundle = jnp.concatenate(
        [right[:slot_total], outgoing[2 * group : 2 * group + slot_total], left[:slot_total]], axis=0
    )
    down_bundle = jnp.concatenate(
        [right[2 * slot_total :], outgoing[2 * group + slot_total :], left[2 * slot_total :]], axis=0
    )
    up = shifted(up_bundle, "prow", -1)
    down = shifted(down_bundle, "prow", 1)
    up, down, finished = lax.optimization_barrier((up, down, finished))
    return jnp.concatenate(
        [down, right[slot_total : 2 * slot_total], left[slot_total : 2 * slot_total], up], axis=0
    ), finished


def per_device(
    dof_values,
    grad_matrix,
    stiff_matrix,
    face_proj,
    face_lift,
    rotate,
    material,
    material_id,
    inv_jacobian,
    normals,
    orientation,
    neighbour,
    neighbour_face,
    send_list,
    recv_list,
):
    elem_count = dof_values.shape[2]
    face_width = face_proj.shape[1]
    face_total = 4 * elem_count
    dtype = dof_values.dtype
    values, wave_speed = element_params(material, material_id, normals)
    face_ids = jnp.arange(face_total, dtype=jnp.int32)
    inside = (neighbour >= 0).reshape(-1)
    local_index = (neighbour_face * elem_count + jnp.maximum(neighbour, 0)).reshape(-1)
    gather_local = ((local_index[None, :] == face_ids[:, None]) & inside[None, :]).astype(dtype)
    source_ids = jnp.concatenate([send_list[0, 0, d : d + 1] for d in SEND_ORDER], axis=0)
    slot_total = source_ids.shape[1]
    gather_out = (source_ids.reshape(-1)[:, None] == face_ids[None, :]).astype(dtype)
    targets = recv_list[0, 0].reshape(-1)
    scatter_in = ((targets[:, None] == face_ids[None, :]) & ~inside[None, :]).astype(dtype)
    current = dof_values
    rotate_negated, half_lift = rotate, face_lift
    slot_chosen = jnp.zeros((3, scatter_in.shape[0]), dtype)
    for time_index in range(STEPS):
        integrated, face_data = local_part(
            current, inv_jacobian, values, grad_matrix, face_proj
        )
        flat_faces = face_data.reshape(9 * face_width, face_total)
        outgoing = lax.dot_general(
            gather_out, flat_faces, (((1,), (1,)), ((), ())), precision=exact_mode
        )

        def local_work(integrated, flat_faces, rotate_negated, half_lift, slot_chosen):
            slopes = jnp.einsum("dab,qbe->dqae", stiff_matrix, integrated, precision=fast_mode)
            volume = star_apply(slopes, inv_jacobian, values)
            if time_index == 0:
                rotate_negated = -rotate_negated
                half_lift = 0.5 * half_lift
                slot_orientation = jnp.dot(
                    scatter_in, orientation.reshape(-1).astype(dtype), precision=exact_mode
                )
                slot_chosen = (
                    slot_orientation[None, :] == jnp.arange(3, dtype=dtype)[:, None]
                ).astype(dtype)
            local_data = jnp.dot(flat_faces, gather_local, precision=exact_mode)
            local_turned = rotate_faces(
                local_data.reshape(9, face_width, 4, elem_count), orientation, rotate_negated
            )
            return volume, local_turned, rotate_negated, half_lift, slot_chosen

        received, (volume, local_turned, rotate_negated, half_lift, slot_chosen) = deliver(
            outgoing,
            slot_total,
            (integrated, flat_faces, rotate_negated, half_lift, slot_chosen),
            local_work,
        )
        remote_turned = lax.dot_general(
            rotate_slots(received, slot_chosen, rotate_negated, face_width),
            scatter_in,
            (((0,), (0,)), ((), ())),
            precision=exact_mode,
        )
        turned_negated = local_turned + remote_turned.reshape(9, face_width, 4, elem_count)
        current = face_update(
            current,
            volume,
            face_data,
            turned_negated,
            normals,
            values,
            wave_speed,
            half_lift,
        )
    return current


def solution(mesh):
    return jax.shard_map(
        per_device,
        mesh=mesh,
        in_specs=(
            P(None, None, ("prow", "pcol")),
            P(),
            P(),
            P(),
            P(),
            P(),
            P(),
            P(("prow", "pcol")),
            P(None, None, ("prow", "pcol")),
            P(None, None, ("prow", "pcol")),
            P(None, ("prow", "pcol")),
            P(None, ("prow", "pcol")),
            P(None, ("prow", "pcol")),
            P("prow", "pcol", None, None),
            P("prow", "pcol", None, None),
        ),
        out_specs=P(None, None, ("prow", "pcol")),
        check_vma=False,
    )
```

```python
import jax
import jax.numpy as jnp
from jax import lax
from jax.sharding import PartitionSpec as P

ORDER = 6
STEPS = 2


exact_mode = lax.Precision.HIGHEST
fast_mode = lax.Precision.HIGH
time_step = 0.8
OFFSETS = ((-1, -1), (-1, 0), (-1, 1), (0, -1), (0, 1), (1, -1), (1, 0), (1, 1))
ENTRIES = (
    (0, 0, 6, 0),
    (0, 1, 6, 1),
    (0, 2, 6, 1),
    (0, 3, 7, 2),
    (0, 5, 8, 2),
    (0, 6, 0, 3),
    (0, 7, 3, 3),
    (0, 8, 5, 3),
    (1, 0, 7, 1),
    (1, 1, 7, 0),
    (1, 2, 7, 1),
    (1, 3, 6, 2),
    (1, 4, 8, 2),
    (1, 6, 3, 3),
    (1, 7, 1, 3),
    (1, 8, 4, 3),
    (2, 0, 8, 1),
    (2, 1, 8, 1),
    (2, 2, 8, 0),
    (2, 4, 7, 2),
    (2, 5, 6, 2),
    (2, 6, 5, 3),
    (2, 7, 4, 3),
    (2, 8, 2, 3),
)


def shifted(x, axis, by):
    devices = lax.axis_size(axis)
    pairs = [(i, i + by) for i in range(devices) if 0 <= i + by < devices]
    return lax.ppermute(x, axis, pairs)


def element_params(material, material_id, normals):
    id_range = jnp.arange(material.shape[0], dtype=jnp.int32)
    chosen = material_id[None, None, :] == id_range[:, None, None]
    params = jnp.sum(jnp.where(chosen, material[:, :, None], 0.0), axis=0)
    density, lame_first, shear_modulus = (params[0], params[1], params[2])
    values = (-(lame_first + 2.0 * shear_modulus), -lame_first, -shear_modulus, -1.0 / density)
    wave_speed = jnp.sqrt((lame_first + 2.0 * shear_modulus) / density) * jnp.sum(
        jnp.abs(normals), axis=1
    )
    return (values, wave_speed)


def elastic_apply(parts, values):
    result = [None] * 9
    for comp_axis, row_index, col_index, kind_index in ENTRIES:
        term = values[kind_index] * parts[comp_axis][col_index]
        result[row_index] = term if result[row_index] is None else result[row_index] + term
    return jnp.stack(result, axis=0)


def star_apply(slopes, inv_jacobian, values):
    parts = [jnp.sum(inv_jacobian[:, k][:, None, None, :] * slopes, axis=0) for k in range(3)]
    return elastic_apply(parts, values)


def predict(current, inv_jacobian, values, grad_matrix):
    derivative = current
    integrated = time_step * current
    factor = time_step
    for power_level in range(1, ORDER):
        slopes = jnp.einsum("dab,qbe->dqae", grad_matrix, derivative, precision=fast_mode)
        derivative = -star_apply(slopes, inv_jacobian, values)
        factor = factor * time_step / (power_level + 1)
        integrated = integrated + factor * derivative
    return integrated


def local_part(current, inv_jacobian, values, grad_matrix, face_proj):
    integrated = predict(current, inv_jacobian, values, grad_matrix)
    face_data = jnp.einsum("fib,qbe->qife", face_proj, integrated, precision=fast_mode)
    return (integrated, face_data)


def face_update(
    current,
    volume,
    face_data,
    neighbour_data,
    orientation,
    normals,
    values,
    wave_speed,
    rotate_negated,
    half_lift,
):
    turned_negated = jnp.einsum(
        "hil,qlfe->hqife", rotate_negated, neighbour_data, precision=fast_mode
    )
    chosen = (orientation[None] == jnp.arange(3, dtype=jnp.int32)[:, None, None]).astype(
        current.dtype
    )
    turned_negated = jnp.sum(turned_negated * chosen[:, None, None, :, :], axis=0)
    both = face_data - turned_negated
    apart = face_data + turned_negated
    parts = [normals[:, k, :][None, None] * both for k in range(3)]
    flux_total = elastic_apply(parts, values) + wave_speed[None, None] * apart
    lifted = jnp.einsum("fai,pife->pae", half_lift, flux_total, precision=fast_mode)
    return current + volume - lifted


SEND_ORDER = (0, 3, 5, 2, 4, 7, 1, 6)


def deliver(outgoing, slot_total, deferred, local_work):
    group = 3 * slot_total
    left = shifted(outgoing[:group], "pcol", -1)
    right = shifted(outgoing[group : 2 * group], "pcol", 1)
    left, right, deferred = lax.optimization_barrier((left, right, deferred))
    finished = local_work(*deferred)
    up_bundle = jnp.concatenate(
        [right[:slot_total], outgoing[2 * group : 2 * group + slot_total], left[:slot_total]], axis=0
    )
    down_bundle = jnp.concatenate(
        [right[2 * slot_total :], outgoing[2 * group + slot_total :], left[2 * slot_total :]], axis=0
    )
    up = shifted(up_bundle, "prow", -1)
    down = shifted(down_bundle, "prow", 1)
    up, down, finished = lax.optimization_barrier((up, down, finished))
    return jnp.concatenate(
        [down, right[slot_total : 2 * slot_total], left[slot_total : 2 * slot_total], up], axis=0
    ), finished


def per_device(
    dof_values,
    grad_matrix,
    stiff_matrix,
    face_proj,
    face_lift,
    rotate,
    material,
    material_id,
    inv_jacobian,
    normals,
    orientation,
    neighbour,
    neighbour_face,
    send_list,
    recv_list,
):
    elem_count = dof_values.shape[2]
    face_width = face_proj.shape[1]
    face_total = 4 * elem_count
    dtype = dof_values.dtype
    values, wave_speed = element_params(material, material_id, normals)
    face_ids = jnp.arange(face_total, dtype=jnp.int32)
    inside = (neighbour >= 0).reshape(-1)
    local_index = (neighbour_face * elem_count + jnp.maximum(neighbour, 0)).reshape(-1)
    gather_local = ((local_index[None, :] == face_ids[:, None]) & inside[None, :]).astype(dtype)
    slot_total = send_list.shape[3]
    natural_out = (send_list.reshape(-1)[:, None] == face_ids[None, :]).astype(dtype)
    slot_ids = jnp.arange(8 * slot_total, dtype=jnp.int32)
    send_slots = (jnp.array(SEND_ORDER, dtype=jnp.int32)[:, None] * slot_total + jnp.arange(slot_total, dtype=jnp.int32)[None, :]).reshape(-1)
    reorder = (send_slots[:, None] == slot_ids[None, :]).astype(dtype)
    gather_out = jnp.dot(reorder, natural_out, precision=exact_mode)
    targets = recv_list[0, 0].reshape(-1)
    scatter_in = ((targets[:, None] == face_ids[None, :]) & ~inside[None, :]).astype(dtype)
    current = dof_values
    rotate_negated, half_lift = rotate, face_lift
    for time_index in range(STEPS):
        integrated, face_data = local_part(
            current, inv_jacobian, values, grad_matrix, face_proj
        )
        flat_faces = face_data.reshape(9 * face_width, face_total)
        outgoing = lax.dot_general(
            gather_out, flat_faces, (((1,), (1,)), ((), ())), precision=exact_mode
        )

        def local_work(integrated, flat_faces, rotate_negated, half_lift):
            slopes = jnp.einsum("dab,qbe->dqae", stiff_matrix, integrated, precision=fast_mode)
            volume = star_apply(slopes, inv_jacobian, values)
            local_data = jnp.dot(flat_faces, gather_local, precision=exact_mode)
            if time_index == 0:
                rotate_negated = -rotate_negated
                half_lift = 0.5 * half_lift
            return volume, local_data, rotate_negated, half_lift

        received, (volume, local_data, rotate_negated, half_lift) = deliver(
            outgoing, slot_total, (integrated, flat_faces, rotate_negated, half_lift), local_work
        )
        neighbour_data = local_data + lax.dot_general(
            received, scatter_in, (((0,), (0,)), ((), ())), precision=exact_mode
        )
        neighbour_data = neighbour_data.reshape(9, face_width, 4, elem_count)
        current = face_update(
            current,
            volume,
            face_data,
            neighbour_data,
            orientation,
            normals,
            values,
            wave_speed,
            rotate_negated,
            half_lift,
        )
    return current


def solution(mesh):
    return jax.shard_map(
        per_device,
        mesh=mesh,
        in_specs=(
            P(None, None, ("prow", "pcol")),
            P(),
            P(),
            P(),
            P(),
            P(),
            P(),
            P(("prow", "pcol")),
            P(None, None, ("prow", "pcol")),
            P(None, None, ("prow", "pcol")),
            P(None, ("prow", "pcol")),
            P(None, ("prow", "pcol")),
            P(None, ("prow", "pcol")),
            P("prow", "pcol", None, None),
            P("prow", "pcol", None, None),
        ),
        out_specs=P(None, None, ("prow", "pcol")),
        check_vma=False,
    )
```

```python
import jax
import jax.numpy as jnp
from jax import lax
from jax.sharding import PartitionSpec as P

ORDER = 6
STEPS = 2


exact_mode = lax.Precision.HIGHEST
fast_mode = lax.Precision.HIGH
time_step = 0.8
OFFSETS = ((-1, -1), (-1, 0), (-1, 1), (0, -1), (0, 1), (1, -1), (1, 0), (1, 1))
ENTRIES = (
    (0, 0, 6, 0),
    (0, 1, 6, 1),
    (0, 2, 6, 1),
    (0, 3, 7, 2),
    (0, 5, 8, 2),
    (0, 6, 0, 3),
    (0, 7, 3, 3),
    (0, 8, 5, 3),
    (1, 0, 7, 1),
    (1, 1, 7, 0),
    (1, 2, 7, 1),
    (1, 3, 6, 2),
    (1, 4, 8, 2),
    (1, 6, 3, 3),
    (1, 7, 1, 3),
    (1, 8, 4, 3),
    (2, 0, 8, 1),
    (2, 1, 8, 1),
    (2, 2, 8, 0),
    (2, 4, 7, 2),
    (2, 5, 6, 2),
    (2, 6, 5, 3),
    (2, 7, 4, 3),
    (2, 8, 2, 3),
)


def shifted(x, axis, by):
    devices = lax.axis_size(axis)
    pairs = [(i, i + by) for i in range(devices) if 0 <= i + by < devices]
    return lax.ppermute(x, axis, pairs)


def element_params(material, material_id, normals):
    id_range = jnp.arange(material.shape[0], dtype=jnp.int32)
    chosen = material_id[None, None, :] == id_range[:, None, None]
    params = jnp.sum(jnp.where(chosen, material[:, :, None], 0.0), axis=0)
    density, lame_first, shear_modulus = (params[0], params[1], params[2])
    values = (-(lame_first + 2.0 * shear_modulus), -lame_first, -shear_modulus, -1.0 / density)
    wave_speed = jnp.sqrt((lame_first + 2.0 * shear_modulus) / density) * jnp.sum(
        jnp.abs(normals), axis=1
    )
    return (values, wave_speed)


def elastic_apply(parts, values):
    result = [None] * 9
    for comp_axis, row_index, col_index, kind_index in ENTRIES:
        term = values[kind_index] * parts[comp_axis][col_index]
        result[row_index] = term if result[row_index] is None else result[row_index] + term
    return jnp.stack(result, axis=0)


def star_apply(slopes, inv_jacobian, values):
    parts = [jnp.sum(inv_jacobian[:, k][:, None, None, :] * slopes, axis=0) for k in range(3)]
    return elastic_apply(parts, values)


def predict(current, inv_jacobian, values, grad_matrix):
    derivative = current
    integrated = time_step * current
    factor = time_step
    for power_level in range(1, ORDER):
        slopes = jnp.einsum("dab,qbe->dqae", grad_matrix, derivative, precision=fast_mode)
        derivative = -star_apply(slopes, inv_jacobian, values)
        factor = factor * time_step / (power_level + 1)
        integrated = integrated + factor * derivative
    return integrated


def local_part(current, inv_jacobian, values, grad_matrix, face_proj):
    integrated = predict(current, inv_jacobian, values, grad_matrix)
    face_data = jnp.einsum("fib,qbe->qife", face_proj, integrated, precision=fast_mode)
    return (integrated, face_data)


def face_update(
    current,
    volume,
    face_data,
    neighbour_data,
    orientation,
    normals,
    values,
    wave_speed,
    rotate_negated,
    half_lift,
):
    turned_negated = jnp.einsum(
        "hil,qlfe->hqife", rotate_negated, neighbour_data, precision=fast_mode
    )
    chosen = (orientation[None] == jnp.arange(3, dtype=jnp.int32)[:, None, None]).astype(
        current.dtype
    )
    turned_negated = jnp.sum(turned_negated * chosen[:, None, None, :, :], axis=0)
    both = face_data - turned_negated
    apart = face_data + turned_negated
    parts = [normals[:, k, :][None, None] * both for k in range(3)]
    flux_total = elastic_apply(parts, values) + wave_speed[None, None] * apart
    lifted = jnp.einsum("fai,pife->pae", half_lift, flux_total, precision=fast_mode)
    return current + volume - lifted


SEND_ORDER = (0, 3, 5, 2, 4, 7, 1, 6)


def deliver(outgoing, slot_total, deferred, local_work):
    group = 3 * slot_total
    left = shifted(outgoing[:group], "pcol", -1)
    right = shifted(outgoing[group : 2 * group], "pcol", 1)
    left, right, deferred = lax.optimization_barrier((left, right, deferred))
    finished = local_work(*deferred)
    up_bundle = jnp.concatenate(
        [right[:slot_total], outgoing[2 * group : 2 * group + slot_total], left[:slot_total]], axis=0
    )
    down_bundle = jnp.concatenate(
        [right[2 * slot_total :], outgoing[2 * group + slot_total :], left[2 * slot_total :]], axis=0
    )
    up = shifted(up_bundle, "prow", -1)
    down = shifted(down_bundle, "prow", 1)
    up, down, finished = lax.optimization_barrier((up, down, finished))
    return jnp.concatenate(
        [down, right[slot_total : 2 * slot_total], left[slot_total : 2 * slot_total], up], axis=0
    ), finished


def per_device(
    dof_values,
    grad_matrix,
    stiff_matrix,
    face_proj,
    face_lift,
    rotate,
    material,
    material_id,
    inv_jacobian,
    normals,
    orientation,
    neighbour,
    neighbour_face,
    send_list,
    recv_list,
):
    elem_count = dof_values.shape[2]
    face_width = face_proj.shape[1]
    face_total = 4 * elem_count
    dtype = dof_values.dtype
    values, wave_speed = element_params(material, material_id, normals)
    face_ids = jnp.arange(face_total, dtype=jnp.int32)
    inside = (neighbour >= 0).reshape(-1)
    local_index = (neighbour_face * elem_count + jnp.maximum(neighbour, 0)).reshape(-1)
    gather_local = ((local_index[None, :] == face_ids[:, None]) & inside[None, :]).astype(dtype)
    source_ids = jnp.concatenate([send_list[0, 0, d : d + 1] for d in SEND_ORDER], axis=0)
    slot_total = source_ids.shape[1]
    gather_out = (source_ids.reshape(-1)[:, None] == face_ids[None, :]).astype(dtype)
    targets = recv_list[0, 0].reshape(-1)
    scatter_in = ((targets[:, None] == face_ids[None, :]) & ~inside[None, :]).astype(dtype)
    current = dof_values
    rotate_negated, half_lift = rotate, face_lift
    for time_index in range(STEPS):
        integrated, face_data = local_part(
            current, inv_jacobian, values, grad_matrix, face_proj
        )
        flat_faces = face_data.reshape(9 * face_width, face_total)
        outgoing = lax.dot_general(
            gather_out, flat_faces, (((1,), (1,)), ((), ())), precision=fast_mode
        )

        def local_work(integrated, flat_faces, rotate_negated, half_lift):
            slopes = jnp.einsum("dab,qbe->dqae", stiff_matrix, integrated, precision=fast_mode)
            volume = star_apply(slopes, inv_jacobian, values)
            local_data = jnp.dot(flat_faces, gather_local, precision=exact_mode)
            if time_index == 0:
                rotate_negated = -rotate_negated
                half_lift = 0.5 * half_lift
            return volume, local_data, rotate_negated, half_lift

        received, (volume, local_data, rotate_negated, half_lift) = deliver(
            outgoing, slot_total, (integrated, flat_faces, rotate_negated, half_lift), local_work
        )
        neighbour_data = local_data + lax.dot_general(
            received, scatter_in, (((0,), (0,)), ((), ())), precision=fast_mode
        )
        neighbour_data = neighbour_data.reshape(9, face_width, 4, elem_count)
        current = face_update(
            current,
            volume,
            face_data,
            neighbour_data,
            orientation,
            normals,
            values,
            wave_speed,
            rotate_negated,
            half_lift,
        )
    return current


def solution(mesh):
    return jax.shard_map(
        per_device,
        mesh=mesh,
        in_specs=(
            P(None, None, ("prow", "pcol")),
            P(),
            P(),
            P(),
            P(),
            P(),
            P(),
            P(("prow", "pcol")),
            P(None, None, ("prow", "pcol")),
            P(None, None, ("prow", "pcol")),
            P(None, ("prow", "pcol")),
            P(None, ("prow", "pcol")),
            P(None, ("prow", "pcol")),
            P("prow", "pcol", None, None),
            P("prow", "pcol", None, None),
        ),
        out_specs=P(None, None, ("prow", "pcol")),
        check_vma=False,
    )
```

```python
import jax
import jax.numpy as jnp
from jax import lax
from jax.sharding import PartitionSpec as P

ORDER = 6
STEPS = 2


exact_mode = lax.Precision.HIGHEST
fast_mode = lax.Precision.HIGH
time_step = 0.8
OFFSETS = ((-1, -1), (-1, 0), (-1, 1), (0, -1), (0, 1), (1, -1), (1, 0), (1, 1))
ENTRIES = (
    (0, 0, 6, 0),
    (0, 1, 6, 1),
    (0, 2, 6, 1),
    (0, 3, 7, 2),
    (0, 5, 8, 2),
    (0, 6, 0, 3),
    (0, 7, 3, 3),
    (0, 8, 5, 3),
    (1, 0, 7, 1),
    (1, 1, 7, 0),
    (1, 2, 7, 1),
    (1, 3, 6, 2),
    (1, 4, 8, 2),
    (1, 6, 3, 3),
    (1, 7, 1, 3),
    (1, 8, 4, 3),
    (2, 0, 8, 1),
    (2, 1, 8, 1),
    (2, 2, 8, 0),
    (2, 4, 7, 2),
    (2, 5, 6, 2),
    (2, 6, 5, 3),
    (2, 7, 4, 3),
    (2, 8, 2, 3),
)


def shifted(x, axis, by):
    devices = lax.axis_size(axis)
    pairs = [(i, i + by) for i in range(devices) if 0 <= i + by < devices]
    return lax.ppermute(x, axis, pairs)


def element_params(material, material_id, normals):
    id_range = jnp.arange(material.shape[0], dtype=jnp.int32)
    chosen = material_id[None, None, :] == id_range[:, None, None]
    params = jnp.sum(jnp.where(chosen, material[:, :, None], 0.0), axis=0)
    density, lame_first, shear_modulus = (params[0], params[1], params[2])
    values = (-(lame_first + 2.0 * shear_modulus), -lame_first, -shear_modulus, -1.0 / density)
    wave_speed = jnp.sqrt((lame_first + 2.0 * shear_modulus) / density) * jnp.sum(
        jnp.abs(normals), axis=1
    )
    return (values, wave_speed)


def elastic_apply(parts, values):
    result = [None] * 9
    for comp_axis, row_index, col_index, kind_index in ENTRIES:
        term = values[kind_index] * parts[comp_axis][col_index]
        result[row_index] = term if result[row_index] is None else result[row_index] + term
    return jnp.stack(result, axis=0)


def star_apply(slopes, inv_jacobian, values):
    parts = [jnp.sum(inv_jacobian[:, k][:, None, None, :] * slopes, axis=0) for k in range(3)]
    return elastic_apply(parts, values)


def predict(current, inv_jacobian, values, grad_matrix):
    derivative = current
    integrated = time_step * current
    factor = time_step
    for power_level in range(1, ORDER):
        slopes = jnp.einsum("dab,qbe->dqae", grad_matrix, derivative, precision=fast_mode)
        derivative = -star_apply(slopes, inv_jacobian, values)
        factor = factor * time_step / (power_level + 1)
        integrated = integrated + factor * derivative
    return integrated


def local_part(current, inv_jacobian, values, grad_matrix, face_proj):
    integrated = predict(current, inv_jacobian, values, grad_matrix)
    face_data = jnp.einsum("fib,qbe->qife", face_proj, integrated, precision=fast_mode)
    return (integrated, face_data)


def face_update(
    current,
    volume,
    face_data,
    neighbour_data,
    orientation,
    normals,
    values,
    wave_speed,
    rotate_negated,
    half_lift,
):
    turned_negated = jnp.einsum(
        "hil,qlfe->hqife", rotate_negated, neighbour_data, precision=fast_mode
    )
    chosen = (orientation[None] == jnp.arange(3, dtype=jnp.int32)[:, None, None]).astype(
        current.dtype
    )
    turned_negated = jnp.sum(turned_negated * chosen[:, None, None, :, :], axis=0)
    both = face_data - turned_negated
    apart = face_data + turned_negated
    parts = [normals[:, k, :][None, None] * both for k in range(3)]
    flux_total = elastic_apply(parts, values) + wave_speed[None, None] * apart
    lifted = jnp.einsum("fai,pife->pae", half_lift, flux_total, precision=fast_mode)
    return current + volume - lifted


SEND_ORDER = (0, 3, 5, 2, 4, 7, 1, 6)


def deliver(outgoing, slot_total, deferred, local_work):
    group = 3 * slot_total
    left = shifted(outgoing[:group], "pcol", -1)
    right = shifted(outgoing[group : 2 * group], "pcol", 1)
    left, right, deferred = lax.optimization_barrier((left, right, deferred))
    finished = local_work(*deferred)
    up_bundle = jnp.concatenate(
        [right[:slot_total], outgoing[2 * group : 2 * group + slot_total], left[:slot_total]], axis=0
    )
    down_bundle = jnp.concatenate(
        [right[2 * slot_total :], outgoing[2 * group + slot_total :], left[2 * slot_total :]], axis=0
    )
    up = shifted(up_bundle, "prow", -1)
    down = shifted(down_bundle, "prow", 1)
    up, down, finished = lax.optimization_barrier((up, down, finished))
    return jnp.concatenate(
        [down, right[slot_total : 2 * slot_total], left[slot_total : 2 * slot_total], up], axis=0
    ), finished


def per_device(
    dof_values,
    grad_matrix,
    stiff_matrix,
    face_proj,
    face_lift,
    rotate,
    material,
    material_id,
    inv_jacobian,
    normals,
    orientation,
    neighbour,
    neighbour_face,
    send_list,
    recv_list,
):
    elem_count = dof_values.shape[2]
    face_width = face_proj.shape[1]
    face_total = 4 * elem_count
    dtype = dof_values.dtype
    values, wave_speed = element_params(material, material_id, normals)
    face_ids = jnp.arange(face_total, dtype=jnp.int32)
    inside = (neighbour >= 0).reshape(-1)
    local_index = (neighbour_face * elem_count + jnp.maximum(neighbour, 0)).reshape(-1)
    gather_local = ((local_index[None, :] == face_ids[:, None]) & inside[None, :]).astype(dtype)
    source_ids = jnp.concatenate([send_list[0, 0, d : d + 1] for d in SEND_ORDER], axis=0)
    slot_total = source_ids.shape[1]
    gather_out = (source_ids.reshape(-1)[:, None] == face_ids[None, :]).astype(dtype)
    targets = recv_list[0, 0].reshape(-1)
    scatter_in = ((targets[:, None] == face_ids[None, :]) & ~inside[None, :]).astype(dtype)
    current = dof_values
    rotate_negated, half_lift = rotate, face_lift
    for time_index in range(STEPS):
        integrated, face_data = local_part(
            current, inv_jacobian, values, grad_matrix, face_proj
        )
        flat_faces = face_data.reshape(9 * face_width, face_total)
        outgoing = lax.dot_general(
            gather_out, flat_faces, (((1,), (1,)), ((), ())), precision=fast_mode
        )

        def local_work(integrated, flat_faces, rotate_negated, half_lift):
            slopes = jnp.einsum("dab,qbe->dqae", stiff_matrix, integrated, precision=fast_mode)
            volume = star_apply(slopes, inv_jacobian, values)
            local_data = jnp.dot(flat_faces, gather_local, precision=exact_mode)
            if time_index == 0:
                rotate_negated = -rotate_negated
                half_lift = 0.5 * half_lift
            return volume, local_data, rotate_negated, half_lift

        received, (volume, local_data, rotate_negated, half_lift) = deliver(
            outgoing, slot_total, (integrated, flat_faces, rotate_negated, half_lift), local_work
        )
        remote_data = jnp.einsum(
            "sqi,sfe->qife",
            received.reshape(-1, 9, face_width),
            scatter_in.reshape(-1, 4, elem_count),
            precision=fast_mode,
        )
        neighbour_data = local_data.reshape(9, face_width, 4, elem_count) + remote_data
        current = face_update(
            current,
            volume,
            face_data,
            neighbour_data,
            orientation,
            normals,
            values,
            wave_speed,
            rotate_negated,
            half_lift,
        )
    return current


def solution(mesh):
    return jax.shard_map(
        per_device,
        mesh=mesh,
        in_specs=(
            P(None, None, ("prow", "pcol")),
            P(),
            P(),
            P(),
            P(),
            P(),
            P(),
            P(("prow", "pcol")),
            P(None, None, ("prow", "pcol")),
            P(None, None, ("prow", "pcol")),
            P(None, ("prow", "pcol")),
            P(None, ("prow", "pcol")),
            P(None, ("prow", "pcol")),
            P("prow", "pcol", None, None),
            P("prow", "pcol", None, None),
        ),
        out_specs=P(None, None, ("prow", "pcol")),
        check_vma=False,
    )
```

```python
import jax
import jax.numpy as jnp
from jax import lax
from jax.sharding import PartitionSpec as P

ORDER = 6
STEPS = 2


exact_mode = lax.Precision.HIGHEST
fast_mode = lax.Precision.HIGH
time_step = 0.8
OFFSETS = ((-1, -1), (-1, 0), (-1, 1), (0, -1), (0, 1), (1, -1), (1, 0), (1, 1))
ENTRIES = (
    (0, 0, 6, 0),
    (0, 1, 6, 1),
    (0, 2, 6, 1),
    (0, 3, 7, 2),
    (0, 5, 8, 2),
    (0, 6, 0, 3),
    (0, 7, 3, 3),
    (0, 8, 5, 3),
    (1, 0, 7, 1),
    (1, 1, 7, 0),
    (1, 2, 7, 1),
    (1, 3, 6, 2),
    (1, 4, 8, 2),
    (1, 6, 3, 3),
    (1, 7, 1, 3),
    (1, 8, 4, 3),
    (2, 0, 8, 1),
    (2, 1, 8, 1),
    (2, 2, 8, 0),
    (2, 4, 7, 2),
    (2, 5, 6, 2),
    (2, 6, 5, 3),
    (2, 7, 4, 3),
    (2, 8, 2, 3),
)


def shifted(x, axis, by):
    devices = lax.axis_size(axis)
    pairs = [(i, i + by) for i in range(devices) if 0 <= i + by < devices]
    return lax.ppermute(x, axis, pairs)


def element_params(material, material_id, normals):
    id_range = jnp.arange(material.shape[0], dtype=jnp.int32)
    onehot = (material_id[None, :] == id_range[:, None]).astype(material.dtype)
    params = jnp.dot(material.T, onehot, precision=fast_mode)
    density, lame_first, shear_modulus = (params[0], params[1], params[2])
    values = (-(lame_first + 2.0 * shear_modulus), -lame_first, -shear_modulus, -1.0 / density)
    wave_speed = jnp.sqrt((lame_first + 2.0 * shear_modulus) / density) * jnp.sum(
        jnp.abs(normals), axis=1
    )
    return (values, wave_speed)


def elastic_apply(parts, values):
    result = [None] * 9
    for comp_axis, row_index, col_index, kind_index in ENTRIES:
        term = values[kind_index] * parts[comp_axis][col_index]
        result[row_index] = term if result[row_index] is None else result[row_index] + term
    return jnp.stack(result, axis=0)


def star_apply(slopes, inv_jacobian, values):
    parts = [jnp.sum(inv_jacobian[:, k][:, None, None, :] * slopes, axis=0) for k in range(3)]
    return elastic_apply(parts, values)


def predict(current, inv_jacobian, values, grad_matrix):
    derivative = current
    integrated = time_step * current
    factor = time_step
    for power_level in range(1, ORDER):
        slopes = jnp.einsum("dab,qbe->dqae", grad_matrix, derivative, precision=fast_mode)
        derivative = -star_apply(slopes, inv_jacobian, values)
        factor = factor * time_step / (power_level + 1)
        integrated = integrated + factor * derivative
    return integrated


def local_part(current, inv_jacobian, values, grad_matrix, face_proj):
    integrated = predict(current, inv_jacobian, values, grad_matrix)
    face_data = jnp.einsum("fib,qbe->qife", face_proj, integrated, precision=fast_mode)
    return (integrated, face_data)


def face_update(
    current,
    volume,
    face_data,
    neighbour_data,
    orientation,
    normals,
    values,
    wave_speed,
    rotate_negated,
    half_lift,
):
    turned_negated = jnp.einsum(
        "hil,qlfe->hqife", rotate_negated, neighbour_data, precision=fast_mode
    )
    chosen = (orientation[None] == jnp.arange(3, dtype=jnp.int32)[:, None, None]).astype(
        current.dtype
    )
    turned_negated = jnp.sum(turned_negated * chosen[:, None, None, :, :], axis=0)
    both = face_data - turned_negated
    apart = face_data + turned_negated
    parts = [normals[:, k, :][None, None] * both for k in range(3)]
    flux_total = elastic_apply(parts, values) + wave_speed[None, None] * apart
    lifted = jnp.einsum("fai,pife->pae", half_lift, flux_total, precision=fast_mode)
    return current + volume - lifted


SEND_ORDER = (0, 3, 5, 2, 4, 7, 1, 6)


def deliver(outgoing, slot_total, deferred, local_work):
    group = 3 * slot_total
    left = shifted(outgoing[:group], "pcol", -1)
    right = shifted(outgoing[group : 2 * group], "pcol", 1)
    left, right, deferred = lax.optimization_barrier((left, right, deferred))
    finished = local_work(*deferred)
    up_bundle = jnp.concatenate(
        [right[:slot_total], outgoing[2 * group : 2 * group + slot_total], left[:slot_total]], axis=0
    )
    down_bundle = jnp.concatenate(
        [right[2 * slot_total :], outgoing[2 * group + slot_total :], left[2 * slot_total :]], axis=0
    )
    up = shifted(up_bundle, "prow", -1)
    down = shifted(down_bundle, "prow", 1)
    up, down, finished = lax.optimization_barrier((up, down, finished))
    return jnp.concatenate(
        [down, right[slot_total : 2 * slot_total], left[slot_total : 2 * slot_total], up], axis=0
    ), finished


def per_device(
    dof_values,
    grad_matrix,
    stiff_matrix,
    face_proj,
    face_lift,
    rotate,
    material,
    material_id,
    inv_jacobian,
    normals,
    orientation,
    neighbour,
    neighbour_face,
    send_list,
    recv_list,
):
    elem_count = dof_values.shape[2]
    face_width = face_proj.shape[1]
    face_total = 4 * elem_count
    dtype = dof_values.dtype
    values, wave_speed = element_params(material, material_id, normals)
    face_ids = jnp.arange(face_total, dtype=jnp.int32)
    inside = (neighbour >= 0).reshape(-1)
    local_index = (neighbour_face * elem_count + jnp.maximum(neighbour, 0)).reshape(-1)
    gather_local = ((local_index[None, :] == face_ids[:, None]) & inside[None, :]).astype(dtype)
    source_ids = jnp.concatenate([send_list[0, 0, d : d + 1] for d in SEND_ORDER], axis=0)
    slot_total = source_ids.shape[1]
    gather_out = (source_ids.reshape(-1)[:, None] == face_ids[None, :]).astype(dtype)
    targets = recv_list[0, 0].reshape(-1)
    scatter_in = ((targets[:, None] == face_ids[None, :]) & ~inside[None, :]).astype(dtype)
    current = dof_values
    rotate_negated, half_lift = rotate, face_lift
    for time_index in range(STEPS):
        integrated, face_data = local_part(
            current, inv_jacobian, values, grad_matrix, face_proj
        )
        flat_faces = face_data.reshape(9 * face_width, face_total)
        outgoing = lax.dot_general(
            gather_out, flat_faces, (((1,), (1,)), ((), ())), precision=fast_mode
        )

        def local_work(integrated, flat_faces, rotate_negated, half_lift):
            slopes = jnp.einsum("dab,qbe->dqae", stiff_matrix, integrated, precision=fast_mode)
            volume = star_apply(slopes, inv_jacobian, values)
            local_data = jnp.dot(flat_faces, gather_local, precision=exact_mode)
            if time_index == 0:
                rotate_negated = -rotate_negated
                half_lift = 0.5 * half_lift
            return volume, local_data, rotate_negated, half_lift

        received, (volume, local_data, rotate_negated, half_lift) = deliver(
            outgoing, slot_total, (integrated, flat_faces, rotate_negated, half_lift), local_work
        )
        neighbour_data = local_data + lax.dot_general(
            received, scatter_in, (((0,), (0,)), ((), ())), precision=fast_mode
        )
        neighbour_data = neighbour_data.reshape(9, face_width, 4, elem_count)
        current = face_update(
            current,
            volume,
            face_data,
            neighbour_data,
            orientation,
            normals,
            values,
            wave_speed,
            rotate_negated,
            half_lift,
        )
    return current


def solution(mesh):
    return jax.shard_map(
        per_device,
        mesh=mesh,
        in_specs=(
            P(None, None, ("prow", "pcol")),
            P(),
            P(),
            P(),
            P(),
            P(),
            P(),
            P(("prow", "pcol")),
            P(None, None, ("prow", "pcol")),
            P(None, None, ("prow", "pcol")),
            P(None, ("prow", "pcol")),
            P(None, ("prow", "pcol")),
            P(None, ("prow", "pcol")),
            P("prow", "pcol", None, None),
            P("prow", "pcol", None, None),
        ),
        out_specs=P(None, None, ("prow", "pcol")),
        check_vma=False,
    )
```

```python
import jax
import jax.numpy as jnp
from jax import lax
from jax.sharding import PartitionSpec as P

ORDER = 6
STEPS = 2


exact_mode = lax.Precision.HIGHEST
fast_mode = lax.Precision.HIGH
time_step = 0.8
OFFSETS = ((-1, -1), (-1, 0), (-1, 1), (0, -1), (0, 1), (1, -1), (1, 0), (1, 1))
ENTRIES = (
    (0, 0, 6, 0),
    (0, 1, 6, 1),
    (0, 2, 6, 1),
    (0, 3, 7, 2),
    (0, 5, 8, 2),
    (0, 6, 0, 3),
    (0, 7, 3, 3),
    (0, 8, 5, 3),
    (1, 0, 7, 1),
    (1, 1, 7, 0),
    (1, 2, 7, 1),
    (1, 3, 6, 2),
    (1, 4, 8, 2),
    (1, 6, 3, 3),
    (1, 7, 1, 3),
    (1, 8, 4, 3),
    (2, 0, 8, 1),
    (2, 1, 8, 1),
    (2, 2, 8, 0),
    (2, 4, 7, 2),
    (2, 5, 6, 2),
    (2, 6, 5, 3),
    (2, 7, 4, 3),
    (2, 8, 2, 3),
)


def shifted(x, axis, by):
    devices = lax.axis_size(axis)
    pairs = [(i, i + by) for i in range(devices) if 0 <= i + by < devices]
    return lax.ppermute(x, axis, pairs)


def element_params(material, material_id, normals):
    id_range = jnp.arange(material.shape[0], dtype=jnp.int32)
    onehot = (material_id[None, :] == id_range[:, None]).astype(material.dtype)
    params = jnp.dot(material.T, onehot, precision=fast_mode)
    density, lame_first, shear_modulus = (params[0], params[1], params[2])
    values = (-(lame_first + 2.0 * shear_modulus), -lame_first, -shear_modulus, -1.0 / density)
    wave_speed = jnp.sqrt((lame_first + 2.0 * shear_modulus) / density) * jnp.sum(
        jnp.abs(normals), axis=1
    )
    return (values, wave_speed)


def elastic_apply(parts, values):
    result = [None] * 9
    for comp_axis, row_index, col_index, kind_index in ENTRIES:
        term = values[kind_index] * parts[comp_axis][col_index]
        result[row_index] = term if result[row_index] is None else result[row_index] + term
    return jnp.stack(result, axis=0)


def star_apply(slopes, inv_jacobian, values):
    parts = [jnp.sum(inv_jacobian[:, k][:, None, None, :] * slopes, axis=0) for k in range(3)]
    return elastic_apply(parts, values)


def predict(current, inv_jacobian, values, grad_matrix):
    derivative = current
    integrated = time_step * current
    factor = time_step
    for power_level in range(1, ORDER):
        slopes = jnp.einsum("dab,qbe->dqae", grad_matrix, derivative, precision=fast_mode)
        derivative = -star_apply(slopes, inv_jacobian, values)
        factor = factor * time_step / (power_level + 1)
        integrated = integrated + factor * derivative
    return integrated


def local_part(current, inv_jacobian, values, grad_matrix, face_proj):
    integrated = predict(current, inv_jacobian, values, grad_matrix)
    face_data = jnp.einsum("fib,qbe->qife", face_proj, integrated, precision=fast_mode)
    return (integrated, face_data)


def face_update(
    current,
    volume,
    face_data,
    neighbour_data,
    orientation,
    normals,
    values,
    wave_speed,
    rotate_negated,
    half_lift,
):
    turned_negated = jnp.einsum(
        "hil,qlfe->hqife", rotate_negated, neighbour_data, precision=fast_mode
    )
    chosen = (orientation[None] == jnp.arange(3, dtype=jnp.int32)[:, None, None]).astype(
        current.dtype
    )
    turned_negated = jnp.sum(turned_negated * chosen[:, None, None, :, :], axis=0)
    both = face_data - turned_negated
    apart = face_data + turned_negated
    parts = [normals[:, k, :][None, None] * both for k in range(3)]
    flux_total = elastic_apply(parts, values) + wave_speed[None, None] * apart
    lifted = jnp.einsum("fai,pife->pae", half_lift, flux_total, precision=fast_mode)
    return current + volume - lifted


SEND_ORDER = (0, 3, 5, 2, 4, 7, 1, 6)


def deliver(outgoing, slot_total, deferred, local_work):
    group = 3 * slot_total
    left = shifted(outgoing[:group], "pcol", -1)
    right = shifted(outgoing[group : 2 * group], "pcol", 1)
    left, right, deferred = lax.optimization_barrier((left, right, deferred))
    finished = local_work(*deferred)
    up_bundle = jnp.concatenate(
        [right[:slot_total], outgoing[2 * group : 2 * group + slot_total], left[:slot_total]], axis=0
    )
    down_bundle = jnp.concatenate(
        [right[2 * slot_total :], outgoing[2 * group + slot_total :], left[2 * slot_total :]], axis=0
    )
    up = shifted(up_bundle, "prow", -1)
    down = shifted(down_bundle, "prow", 1)
    up, down, finished = lax.optimization_barrier((up, down, finished))
    return jnp.concatenate(
        [down, right[slot_total : 2 * slot_total], left[slot_total : 2 * slot_total], up], axis=0
    ), finished


def per_device(
    dof_values,
    grad_matrix,
    stiff_matrix,
    face_proj,
    face_lift,
    rotate,
    material,
    material_id,
    inv_jacobian,
    normals,
    orientation,
    neighbour,
    neighbour_face,
    send_list,
    recv_list,
):
    elem_count = dof_values.shape[2]
    face_width = face_proj.shape[1]
    face_total = 4 * elem_count
    dtype = dof_values.dtype
    values, wave_speed = element_params(material, material_id, normals)
    face_ids = jnp.arange(face_total, dtype=jnp.int32)
    inside = (neighbour >= 0).reshape(-1)
    local_index = (neighbour_face * elem_count + jnp.maximum(neighbour, 0)).reshape(-1)
    gather_local = ((local_index[None, :] == face_ids[:, None]) & inside[None, :]).astype(dtype)
    slot_total = send_list.shape[3]
    slot_ids = jnp.arange(8 * slot_total, dtype=jnp.int32)
    send_slots = jnp.array(
        [d * slot_total + m for d in SEND_ORDER for m in range(slot_total)], dtype=jnp.int32
    )
    reorder = (send_slots[:, None] == slot_ids[None, :]).astype(dtype)
    source_ids = jnp.dot(reorder, send_list.reshape(-1).astype(dtype), precision=exact_mode)
    gather_out = (source_ids[:, None] == face_ids.astype(dtype)[None, :]).astype(dtype)
    targets = recv_list[0, 0].reshape(-1)
    scatter_in = ((targets[:, None] == face_ids[None, :]) & ~inside[None, :]).astype(dtype)
    current = dof_values
    rotate_negated, half_lift = rotate, face_lift
    for time_index in range(STEPS):
        integrated, face_data = local_part(
            current, inv_jacobian, values, grad_matrix, face_proj
        )
        flat_faces = face_data.reshape(9 * face_width, face_total)
        outgoing = lax.dot_general(
            gather_out, flat_faces, (((1,), (1,)), ((), ())), precision=fast_mode
        )

        def local_work(integrated, flat_faces, rotate_negated, half_lift):
            slopes = jnp.einsum("dab,qbe->dqae", stiff_matrix, integrated, precision=fast_mode)
            volume = star_apply(slopes, inv_jacobian, values)
            local_data = jnp.dot(flat_faces, gather_local, precision=exact_mode)
            if time_index == 0:
                rotate_negated = -rotate_negated
                half_lift = 0.5 * half_lift
            return volume, local_data, rotate_negated, half_lift

        received, (volume, local_data, rotate_negated, half_lift) = deliver(
            outgoing, slot_total, (integrated, flat_faces, rotate_negated, half_lift), local_work
        )
        neighbour_data = local_data + lax.dot_general(
            received, scatter_in, (((0,), (0,)), ((), ())), precision=fast_mode
        )
        neighbour_data = neighbour_data.reshape(9, face_width, 4, elem_count)
        current = face_update(
            current,
            volume,
            face_data,
            neighbour_data,
            orientation,
            normals,
            values,
            wave_speed,
            rotate_negated,
            half_lift,
        )
    return current


def solution(mesh):
    return jax.shard_map(
        per_device,
        mesh=mesh,
        in_specs=(
            P(None, None, ("prow", "pcol")),
            P(),
            P(),
            P(),
            P(),
            P(),
            P(),
            P(("prow", "pcol")),
            P(None, None, ("prow", "pcol")),
            P(None, None, ("prow", "pcol")),
            P(None, ("prow", "pcol")),
            P(None, ("prow", "pcol")),
            P(None, ("prow", "pcol")),
            P("prow", "pcol", None, None),
            P("prow", "pcol", None, None),
        ),
        out_specs=P(None, None, ("prow", "pcol")),
        check_vma=False,
    )
```
